32 devices in a mesh: dp: 4 (over z), expert: 8 (over y, x, core).
Axes of the slice: x: 2, y: 2, z: 4, core: 2. Of those that a mesh axis runs over, the one named last changes fastest.
Arguments:
- tokens: bfloat16 [384, 4096], P('expert', 'dp'), may hold values from -6 to 6
- out_grad: bfloat16 [384, 4096], P('expert', 'dp'), may hold values from -6 to 6
- expert_ids: int32 [384, 8], P('expert'), may hold values from 0 to 63, all different within a row; in each aligned block of 48 rows (0 to 47, 48 to 95, ...) at most 12 rows name the same one
- route_weights: float32 [384, 8], P('expert'), may hold values from 0.05 to 1
- gate_weight: bfloat16 [64, 4096, 768], P('expert', 'dp'), may hold values from -0.09375 to 0.09375
- up_weight: bfloat16 [64, 4096, 768], P('expert', 'dp'), may hold values from -0.09375 to 0.09375
- down_weight: bfloat16 [64, 768, 4096], P('expert', None, 'dp'), may hold values from -0.21875 to 0.21875
Outputs:
- layer_out: bfloat16 [384, 4096], P('expert', 'dp')
- grad_tokens: bfloat16 [384, 4096], P('expert', 'dp')
- gate_grad: bfloat16 [64, 4096, 768], P('expert', 'dp')
- up_grad: bfloat16 [64, 4096, 768], P('expert', 'dp')
- down_grad: bfloat16 [64, 768, 4096], P('expert', None, 'dp')
The draws below stay inside these ranges and needn't reach their ends.
Inputs may be any that keep to these rules, and one draw needn't show every extreme that they name: `expert_ids`: each row names 8 different experts. In the 48 rows of one index of the expert axis no expert is named more than 12 times, and in every draw some expert is named exactly 12 times there.
All inputs are finite; a program needn't handle non-finite values.
Results may differ from the reference program's by a relative error of at most 0.029.
Values may be sent and summed in bfloat16 or wider, within the bound.
No kernel may reach another device: no remote copies, remote signals or barrier semaphores. Data moves between devices by JAX's collectives and lax.ppermute only.
A program may use at most 128 MiB of HBM per device.

```python
import math
import jax
import jax.numpy as jnp
import numpy as np
from jax import lax

D = 4096
FF = 768
EXPERTS = 64
TOP = 8
TOK_DEV = 48
TOKENS = 384
CAP = 12
N_DP = 4
N_EXPERT = 8


def shard_levels(own_key, shape, split, least, high):
    gain, own = 1.0, jax.random.fold_in(own_key, 6)
    for axis_at, blocks in split:
        steps = jnp.exp(jax.random.uniform(jax.random.fold_in(own, axis_at), (blocks,), jnp.float32, least / len(split), high / len(split)))
        gain = gain * jnp.repeat(steps, shape[axis_at] // blocks).reshape([-1 if axis == axis_at else 1 for axis in range(len(shape))])
    return gain


def shared_out(key, own, number, rows, number_of, top, bound, lean):
    ranking = jax.random.permutation(key, number_of)
    packed, usual = load_shares(number_of, rows * top, bound, lean, True), load_shares(number_of, rows * top, bound, lean, False)
    places = jnp.arange(number_of)

    def named(tallies, turn):
        used = int((tallies > 0).sum())
        fixed = max(1, used // 4)
        passed = fixed + (places - fixed + turn * (used - fixed)) % max(1, number_of - fixed)
        return jnp.zeros((number_of,), jnp.int32).at[ranking[jnp.where(places < fixed, places, passed)]].set(jnp.asarray(tallies, jnp.int32))

    tallies = jnp.where(number % 4 == 0, named(packed, number // 4), named(usual, number - number // 4 - 1))
    mixed = jax.random.permutation(jax.random.fold_in(own, 3), number_of)
    donor, taker = mixed[0:number_of // 2 * 2:2], mixed[1:number_of // 2 * 2:2]
    room = jnp.minimum(tallies[donor] - 1, bound - tallies[taker]) // 2
    room = jnp.where((donor == ranking[0]) | (taker == ranking[0]) | (tallies[taker] == 0), 0, jnp.maximum(room, 0))
    passed = jax.random.randint(jax.random.fold_in(own, 4), (number_of // 2,), 0, 1 << 20) % (room + 1)
    tallies = tallies.at[donor].add(-passed).at[taker].add(passed)
    members = jnp.searchsorted(jnp.cumsum(tallies), jnp.arange(rows * top), side="right").astype(jnp.int32)
    listing = members.reshape(top, rows).T
    listing = listing[jax.random.permutation(jax.random.fold_in(own, 1), rows)]
    turn = jax.random.randint(jax.random.fold_in(own, 2), (rows, 1), 0, top)
    return jnp.take_along_axis(listing, (jnp.arange(top)[None, :] + turn) % top, axis=1)


def load_shares(amount, total, limit, slope, full):
    loads = [(1 << 20) // math.isqrt(rank ** slope) + 1 for rank in range(1, amount + 1)]
    largest = limit if full else min(limit, max(-(-total // amount), total * loads[0] // sum(loads)))
    least = 1 if total - largest >= amount - 1 else 0
    holding, rest = [largest] + [least] * (amount - 1), total - largest - least * (amount - 1)
    while rest > 0:
        free = [i for i in range(1, amount) if holding[i] < largest] or [i for i in range(1, amount) if holding[i] < limit]
        whole, left = sum([loads[i] for i in free]), rest
        for i in free:
            addition = min(limit - holding[i], max(1, left * loads[i] // whole), rest)
            holding[i] = holding[i] + addition
            rest = rest - addition
    return np.array(holding)


def scatter_about(rng, extent, spread, reach, shards=(), held_as=jnp.bfloat16):
    array = jax.random.normal(rng, extent, jnp.float32) * spread
    if len(shards) > 0:
        array = shard_levels(rng, extent, shards, -0.22, 0.18) * array
    return jnp.clip(array, min=-reach, max=reach).astype(held_as)


def setup_inputs(seed: int = 0) -> dict:
    seeds = jax.random.split(jax.random.key(seed), 8)
    tokens = scatter_about(seeds[0], (TOKENS, D), 1.0, 6.0, ((0, 8), (1, 4)))
    out_grad = scatter_about(seeds[1], (TOKENS, D), 1.0, 6.0, ((0, 8), (1, 4)))
    expert_ids_keys = jax.random.split(jax.random.fold_in(seeds[2], 1), TOKENS // TOK_DEV)
    expert_ids_turns = jax.random.permutation(jax.random.fold_in(seeds[2], 3), TOKENS // TOK_DEV)
    expert_ids = jax.vmap(lambda own, number: shared_out(jax.random.fold_in(seeds[2], 2), own, number, TOK_DEV, EXPERTS, TOP, CAP, 2))(expert_ids_keys, expert_ids_turns).reshape((TOKENS, TOP))
    route_weights = jnp.clip(jnp.exp(math.log(1.0) - 2.9957323 * jax.random.uniform(seeds[3], (TOKENS, TOP), jnp.float32) ** shard_levels(seeds[3], (TOKENS, TOP), ((0, 8),), -0.2, 0.2)), 0.05, 1.0)
    gate_weight = scatter_about(seeds[4], (EXPERTS, D, FF), D ** -0.5, 0.09375, ((0, 8), (1, 4)))
    up_weight = scatter_about(seeds[5], (EXPERTS, D, FF), D ** -0.5, 0.09375, ((0, 8), (1, 4)))
    down_weight = scatter_about(seeds[6], (EXPERTS, FF, D), FF ** -0.5, 0.21875, ((0, 8), (2, 4)))
    return dict(tokens=tokens, out_grad=out_grad, expert_ids=expert_ids, route_weights=route_weights, gate_weight=gate_weight, up_weight=up_weight, down_weight=down_weight)


def split_sum(left, right, pattern):
    parts = jnp.einsum(pattern, left, right, precision=lax.Precision.HIGHEST)
    parts = lax.optimization_barrier(parts.astype(jnp.bfloat16)).astype(jnp.float32)
    return jnp.sum(parts, axis=0)


def reference(tokens, out_grad, expert_ids, route_weights, gate_weight, up_weight, down_weight):
    slot_count = TOK_DEV * TOP
    flat_ids = expert_ids.reshape(N_EXPERT, slot_count)
    onehot = (flat_ids[:, :, None] == jnp.arange(EXPERTS, dtype=jnp.int32)[None, None, :]).astype(jnp.int32)
    before = jnp.cumsum(onehot, axis=1) - onehot
    slot_rank = jnp.sum(before * onehot, axis=2).astype(jnp.int32)
    source = jnp.arange(N_EXPERT, dtype=jnp.int32)[:, None]
    slot_place = ((flat_ids * N_EXPERT + source) * CAP + slot_rank).reshape(-1).astype(jnp.int32)
    total_rows = EXPERTS * N_EXPERT * CAP
    token_of = (jnp.arange(TOKENS * TOP, dtype=jnp.int32) // TOP).astype(jnp.int32)
    holder = jnp.full((total_rows,), TOKENS, jnp.int32).at[slot_place].set(token_of)
    weight_of = jnp.zeros((total_rows,), jnp.float32).at[slot_place].set(route_weights.reshape(-1))
    padded_tokens = jnp.concatenate([tokens, jnp.zeros((1, D), jnp.bfloat16)], axis=0)
    padded_grad = jnp.concatenate([out_grad, jnp.zeros((1, D), jnp.bfloat16)], axis=0)
    rows_each = N_EXPERT * CAP
    holder_rows = holder.reshape(EXPERTS, rows_each)
    weight_rows = weight_of.reshape(EXPERTS, rows_each)
    highest = lax.Precision.HIGHEST
    group_width = D // N_DP

    def one_expert(items):
        rows, weights, gate_w, up_w, down_w = items
        x_in = padded_tokens[rows].astype(jnp.float32)
        dy_in = (weights[:, None] * padded_grad[rows].astype(jnp.float32)).astype(jnp.bfloat16).astype(jnp.float32)
        gate_f = gate_w.astype(jnp.float32)
        up_f = up_w.astype(jnp.float32)
        down_f = down_w.astype(jnp.float32)
        x_split = x_in.reshape(rows_each, N_DP, group_width)
        dy_split = dy_in.reshape(rows_each, N_DP, group_width)
        gate_sum = split_sum(x_split, gate_f.reshape(N_DP, group_width, FF), "rjd,jdf->jrf")
        up_sum = split_sum(x_split, up_f.reshape(N_DP, group_width, FF), "rjd,jdf->jrf")
        back_sum = split_sum(dy_split, down_f.reshape(FF, N_DP, group_width), "rjd,fjd->jrf")
        logistic = jax.nn.sigmoid(gate_sum)
        activated = gate_sum * logistic
        hidden = (activated * up_sum).astype(jnp.bfloat16).astype(jnp.float32)
        gate_delta = (back_sum * up_sum * logistic * (1.0 + gate_sum * (1.0 - logistic))).astype(jnp.bfloat16).astype(jnp.float32)
        up_delta = (back_sum * activated).astype(jnp.bfloat16).astype(jnp.float32)
        expert_out = jnp.dot(hidden, down_f, precision=highest).astype(jnp.bfloat16)
        expert_back = (jnp.dot(gate_delta, gate_f.T, precision=highest) + jnp.dot(up_delta, up_f.T, precision=highest)).astype(jnp.bfloat16)
        gate_g = jnp.dot(x_in.T, gate_delta, precision=highest).astype(jnp.bfloat16)
        up_g = jnp.dot(x_in.T, up_delta, precision=highest).astype(jnp.bfloat16)
        down_g = jnp.dot(hidden.T, dy_in, precision=highest).astype(jnp.bfloat16)
        return expert_out, expert_back, gate_g, up_g, down_g

    expert_out, expert_back, gate_grad, up_grad, down_grad = lax.map(
        one_expert, (holder_rows, weight_rows, gate_weight, up_weight, down_weight))
    out_flat = expert_out.reshape(total_rows, D)
    back_flat = expert_back.reshape(total_rows, D)
    places = slot_place.reshape(TOKENS, TOP)
    picked_out = jnp.take(out_flat, places, axis=0).astype(jnp.float32)
    layer_out = jnp.sum(picked_out * route_weights[:, :, None], axis=1).astype(jnp.bfloat16)
    picked_back = jnp.take(back_flat, places, axis=0).astype(jnp.float32)
    grad_tokens = jnp.sum(picked_back, axis=1).astype(jnp.bfloat16)
    return layer_out, grad_tokens, gate_grad, up_grad, down_grad
```

```python
import jax
import jax.numpy as jnp
from jax import lax
from jax.sharding import PartitionSpec as P


def swiglu_parts(gate_sum, up_sum, back_sum):
    logistic = jax.nn.sigmoid(gate_sum)
    activated = gate_sum * logistic
    hidden = (activated * up_sum).astype(jnp.bfloat16)
    gate_delta = (back_sum * up_sum * logistic * (1.0 + gate_sum * (1.0 - logistic))).astype(
        jnp.bfloat16
    )
    up_delta = (back_sum * activated).astype(jnp.bfloat16)
    return (hidden, gate_delta, up_delta)


def local(tokens, out_grad, expert_ids, route_weights, gate_weight, up_weight, down_weight):
    token_count, width_dev = tokens.shape
    per_token = expert_ids.shape[1]
    local_experts = gate_weight.shape[0]
    hidden_units = gate_weight.shape[2]
    sources = lax.axis_size("expert")
    experts = local_experts * sources
    capacity = 2 * token_count * per_token // experts
    slot_count = token_count * per_token
    me = lax.axis_index("expert")

    feats = lax.all_gather(
        jnp.concatenate([tokens, out_grad], axis=1), "expert", axis=0, tiled=True
    )
    ids_all = lax.all_gather(expert_ids, "expert", axis=0, tiled=True)
    w_all = lax.all_gather(route_weights, "expert", axis=0, tiled=True)
    all_tokens = sources * token_count

    flat_all = ids_all.reshape(sources, slot_count)
    position = jnp.arange(slot_count, dtype=jnp.int32)
    earlier = (flat_all[:, None, :] == flat_all[:, :, None]) & (
        position[None, None, :] < position[None, :, None]
    )
    rank_all = jnp.sum(earlier.astype(jnp.int32), axis=2)
    local_e = flat_all - me * local_experts
    is_local = (local_e >= 0) & (local_e < local_experts)
    src = jnp.arange(sources, dtype=jnp.int32)[:, None]
    row_count = local_experts * sources * capacity
    row_of = jnp.where(is_local, (local_e * sources + src) * capacity + rank_all, row_count)
    row_of = row_of.reshape(sources * slot_count)
    token_of = jnp.arange(sources * slot_count, dtype=jnp.int32) // per_token
    target = jnp.arange(row_count, dtype=jnp.int32)
    hit = target[:, None] == row_of[None, :]
    holder = jnp.sum(jnp.where(hit, token_of[None, :] + 1, 0), axis=1) - 1
    row_weight = jnp.sum(jnp.where(hit, w_all.reshape(-1)[None, :], 0.0), axis=1)
    select = (holder[:, None] == jnp.arange(all_tokens, dtype=jnp.int32)[None, :]).astype(
        jnp.bfloat16
    )
    picked = jnp.dot(select, feats, preferred_element_type=jnp.float32)
    x_in = picked[:, :width_dev].astype(jnp.bfloat16)
    dy_in = (row_weight[:, None] * picked[:, width_dev:]).astype(jnp.bfloat16)
    x_in = x_in.reshape(local_experts, sources * capacity, width_dev)
    dy_in = dy_in.reshape(local_experts, sources * capacity, width_dev)

    gate_part = jnp.einsum(
        "jrd,jdf->jrf", x_in, gate_weight, preferred_element_type=jnp.float32
    ).astype(jnp.bfloat16)
    up_part = jnp.einsum(
        "jrd,jdf->jrf", x_in, up_weight, preferred_element_type=jnp.float32
    ).astype(jnp.bfloat16)
    back_part = jnp.einsum(
        "jrd,jfd->jrf", dy_in, down_weight, preferred_element_type=jnp.float32
    ).astype(jnp.bfloat16)
    parts = jnp.concatenate([gate_part, up_part, back_part], axis=2).reshape(
        row_count, 3 * hidden_units
    )
    sums = lax.psum_scatter(parts, "dp", scatter_dimension=0, tiled=True).astype(jnp.float32)
    hidden, gate_delta, up_delta = swiglu_parts(
        sums[:, :hidden_units],
        sums[:, hidden_units : 2 * hidden_units],
        sums[:, 2 * hidden_units :],
    )
    acts = lax.all_gather(
        jnp.concatenate([hidden, gate_delta, up_delta], axis=1), "dp", axis=0, tiled=True
    )
    expert_shape = (local_experts, sources, capacity, hidden_units)
    hidden = acts[:, :hidden_units].reshape(expert_shape)
    gate_delta = acts[:, hidden_units : 2 * hidden_units].reshape(expert_shape)
    up_delta = acts[:, 2 * hidden_units :].reshape(expert_shape)
    in_tokens = x_in.reshape(local_experts, sources, capacity, width_dev)
    in_grads = dy_in.reshape(local_experts, sources, capacity, width_dev)

    expert_out = jnp.einsum(
        "jscf,jfd->sjcd", hidden, down_weight, preferred_element_type=jnp.float32
    ).astype(jnp.bfloat16)
    expert_back = (
        jnp.einsum("jscf,jdf->sjcd", gate_delta, gate_weight, preferred_element_type=jnp.float32)
        + jnp.einsum("jscf,jdf->sjcd", up_delta, up_weight, preferred_element_type=jnp.float32)
    ).astype(jnp.bfloat16)
    gate_grad = jnp.einsum(
        "jscd,jscf->jdf", in_tokens, gate_delta, preferred_element_type=jnp.float32
    ).astype(jnp.bfloat16)
    up_grad = jnp.einsum(
        "jscd,jscf->jdf", in_tokens, up_delta, preferred_element_type=jnp.float32
    ).astype(jnp.bfloat16)
    down_grad = jnp.einsum(
        "jscf,jscd->jfd", hidden, in_grads, preferred_element_type=jnp.float32
    ).astype(jnp.bfloat16)

    buffer_rows = experts * capacity
    both = jnp.concatenate([expert_out, expert_back], axis=3).reshape(
        buffer_rows, 2 * width_dev
    )
    back_rows = lax.all_to_all(both, "expert", split_axis=0, concat_axis=0, tiled=True)

    flat_ids = expert_ids.reshape(slot_count)
    earlier_local = (flat_ids[None, :] == flat_ids[:, None]) & (
        position[None, :] < position[:, None]
    )
    slot_rank = jnp.sum(earlier_local.astype(jnp.int32), axis=1)
    slot_place = (flat_ids * capacity + slot_rank).reshape(token_count, per_token)
    picked_rows = jnp.take(back_rows, slot_place, axis=0).astype(jnp.float32)
    layer_out = jnp.sum(
        picked_rows[:, :, :width_dev] * route_weights[:, :, None], axis=1
    ).astype(jnp.bfloat16)
    grad_tokens = jnp.sum(picked_rows[:, :, width_dev:], axis=1).astype(jnp.bfloat16)
    return (layer_out, grad_tokens, gate_grad, up_grad, down_grad)


def solution(mesh):
    in_specs = (
        P("expert", "dp"),
        P("expert", "dp"),
        P("expert", None),
        P("expert", None),
        P("expert", "dp", None),
        P("expert", "dp", None),
        P("expert", None, "dp"),
    )
    out_specs = (
        P("expert", "dp"),
        P("expert", "dp"),
        P("expert", "dp", None),
        P("expert", "dp", None),
        P("expert", None, "dp"),
    )
    return jax.shard_map(local, mesh=mesh, in_specs=in_specs, out_specs=out_specs, check_vma=False)
```

```python
import jax
import jax.numpy as jnp
from jax import lax
from jax.sharding import PartitionSpec as P


def swiglu_parts(gate_sum, up_sum, back_sum):
    logistic = jax.nn.sigmoid(gate_sum)
    activated = gate_sum * logistic
    hidden = (activated * up_sum).astype(jnp.bfloat16)
    gate_delta = (back_sum * up_sum * logistic * (1.0 + gate_sum * (1.0 - logistic))).astype(
        jnp.bfloat16
    )
    up_delta = (back_sum * activated).astype(jnp.bfloat16)
    return (hidden, gate_delta, up_delta)


def split_f32(value):
    high = value.astype(jnp.bfloat16)
    rest = value - high.astype(jnp.float32)
    middle = rest.astype(jnp.bfloat16)
    low = (rest - middle.astype(jnp.float32)).astype(jnp.bfloat16)
    return high, middle, low


def local(tokens, out_grad, expert_ids, route_weights, gate_weight, up_weight, down_weight):
    token_count, width_dev = tokens.shape
    per_token = expert_ids.shape[1]
    local_experts = gate_weight.shape[0]
    hidden_units = gate_weight.shape[2]
    sources = lax.axis_size("expert")
    experts = local_experts * sources
    capacity = 2 * token_count * per_token // experts
    slot_count = token_count * per_token
    me = lax.axis_index("expert")

    high, middle, low = split_f32(route_weights)
    route_cols = 4 * per_token
    pad_cols = (-route_cols) % 128
    packed = jnp.concatenate(
        [
            tokens,
            out_grad,
            expert_ids.astype(jnp.bfloat16),
            high,
            middle,
            low,
            jnp.zeros((token_count, pad_cols), jnp.bfloat16),
        ],
        axis=1,
    )
    gathered = lax.all_gather(packed, "expert", axis=0, tiled=True)
    feats = gathered[:, : 2 * width_dev]
    route_all = gathered[:, 2 * width_dev : 2 * width_dev + route_cols].astype(jnp.float32)
    ids_all = route_all[:, :per_token].astype(jnp.int32)
    w_all = (
        route_all[:, per_token : 2 * per_token] + route_all[:, 2 * per_token : 3 * per_token]
    ) + route_all[:, 3 * per_token :]
    all_tokens = sources * token_count

    flat_all = ids_all.reshape(sources, slot_count)
    position = jnp.arange(slot_count, dtype=jnp.int32)
    earlier = (flat_all[:, None, :] == flat_all[:, :, None]) & (
        position[None, None, :] < position[None, :, None]
    )
    rank_all = jnp.sum(earlier.astype(jnp.int32), axis=2)
    local_e = flat_all - me * local_experts
    is_local = (local_e >= 0) & (local_e < local_experts)
    src = jnp.arange(sources, dtype=jnp.int32)[:, None]
    row_count = local_experts * sources * capacity
    row_of = jnp.where(is_local, (local_e * sources + src) * capacity + rank_all, row_count)
    row_of = row_of.reshape(sources * slot_count)
    token_of = jnp.arange(sources * slot_count, dtype=jnp.int32) // per_token
    target = jnp.arange(row_count, dtype=jnp.int32)
    hit = target[:, None] == row_of[None, :]
    holder = jnp.sum(jnp.where(hit, token_of[None, :] + 1, 0), axis=1) - 1
    row_weight = jnp.sum(jnp.where(hit, w_all.reshape(-1)[None, :], 0.0), axis=1)
    select = (holder[:, None] == jnp.arange(all_tokens, dtype=jnp.int32)[None, :]).astype(
        jnp.bfloat16
    )
    picked = jnp.dot(select, feats, preferred_element_type=jnp.float32)
    x_in = picked[:, :width_dev].astype(jnp.bfloat16)
    dy_in = (row_weight[:, None] * picked[:, width_dev:]).astype(jnp.bfloat16)
    x_in = x_in.reshape(local_experts, sources * capacity, width_dev)
    dy_in = dy_in.reshape(local_experts, sources * capacity, width_dev)

    chunks = 2 if local_experts % 2 == 0 else 1
    per_chunk = local_experts // chunks
    chunk_rows = per_chunk * sources * capacity
    spans = [slice(h * per_chunk, (h + 1) * per_chunk) for h in range(chunks)]

    reduced = []
    for span in spans:
        x_c, dy_c = x_in[span], dy_in[span]
        gate_part = jnp.einsum(
            "jrd,jdf->jrf", x_c, gate_weight[span], preferred_element_type=jnp.float32
        ).astype(jnp.bfloat16)
        up_part = jnp.einsum(
            "jrd,jdf->jrf", x_c, up_weight[span], preferred_element_type=jnp.float32
        ).astype(jnp.bfloat16)
        back_part = jnp.einsum(
            "jrd,jfd->jrf", dy_c, down_weight[span], preferred_element_type=jnp.float32
        ).astype(jnp.bfloat16)
        parts = jnp.concatenate([gate_part, up_part, back_part], axis=2).reshape(
            chunk_rows, 3 * hidden_units
        )
        reduced.append(lax.psum_scatter(parts, "dp", scatter_dimension=0, tiled=True))

    gathered_acts = []
    for sums in reduced:
        sums = sums.astype(jnp.float32)
        hidden, gate_delta, up_delta = swiglu_parts(
            sums[:, :hidden_units],
            sums[:, hidden_units : 2 * hidden_units],
            sums[:, 2 * hidden_units :],
        )
        gathered_acts.append(
            lax.all_gather(
                jnp.concatenate([hidden, gate_delta, up_delta], axis=1), "dp", axis=0, tiled=True
            )
        )

    chunk_shape = (per_chunk, sources, capacity, hidden_units)
    returned = []
    acts_all = []
    for span, acts in zip(spans, gathered_acts):
        hidden = acts[:, :hidden_units].reshape(chunk_shape)
        gate_delta = acts[:, hidden_units : 2 * hidden_units].reshape(chunk_shape)
        up_delta = acts[:, 2 * hidden_units :].reshape(chunk_shape)
        acts_all.append((hidden, gate_delta, up_delta))
        expert_out = jnp.einsum(
            "jscf,jfd->sjcd", hidden, down_weight[span], preferred_element_type=jnp.float32
        ).astype(jnp.bfloat16)
        expert_back = (
            jnp.einsum(
                "jscf,jdf->sjcd", gate_delta, gate_weight[span], preferred_element_type=jnp.float32
            )
            + jnp.einsum(
                "jscf,jdf->sjcd", up_delta, up_weight[span], preferred_element_type=jnp.float32
            )
        ).astype(jnp.bfloat16)
        both = jnp.concatenate([expert_out, expert_back], axis=3).reshape(
            sources * per_chunk * capacity, 2 * width_dev
        )
        returned.append(
            lax.all_to_all(both, "expert", split_axis=0, concat_axis=0, tiled=True).reshape(
                sources, per_chunk, capacity, 2 * width_dev
            )
        )

    hidden = jnp.concatenate([a[0] for a in acts_all], axis=0)
    gate_delta = jnp.concatenate([a[1] for a in acts_all], axis=0)
    up_delta = jnp.concatenate([a[2] for a in acts_all], axis=0)
    in_tokens = x_in.reshape(local_experts, sources, capacity, width_dev)
    in_grads = dy_in.reshape(local_experts, sources, capacity, width_dev)
    gate_grad = jnp.einsum(
        "jscd,jscf->jdf", in_tokens, gate_delta, preferred_element_type=jnp.float32
    ).astype(jnp.bfloat16)
    up_grad = jnp.einsum(
        "jscd,jscf->jdf", in_tokens, up_delta, preferred_element_type=jnp.float32
    ).astype(jnp.bfloat16)
    down_grad = jnp.einsum(
        "jscf,jscd->jfd", hidden, in_grads, preferred_element_type=jnp.float32
    ).astype(jnp.bfloat16)

    back_rows = jnp.concatenate(returned, axis=1).reshape(experts * capacity, 2 * width_dev)
    flat_ids = expert_ids.reshape(slot_count)
    earlier_local = (flat_ids[None, :] == flat_ids[:, None]) & (
        position[None, :] < position[:, None]
    )
    slot_rank = jnp.sum(earlier_local.astype(jnp.int32), axis=1)
    slot_place = (flat_ids * capacity + slot_rank).reshape(token_count, per_token)
    picked_rows = jnp.take(back_rows, slot_place, axis=0).astype(jnp.float32)
    layer_out = jnp.sum(
        picked_rows[:, :, :width_dev] * route_weights[:, :, None], axis=1
    ).astype(jnp.bfloat16)
    grad_tokens = jnp.sum(picked_rows[:, :, width_dev:], axis=1).astype(jnp.bfloat16)
    return (layer_out, grad_tokens, gate_grad, up_grad, down_grad)


def solution(mesh):
    in_specs = (
        P("expert", "dp"),
        P("expert", "dp"),
        P("expert", None),
        P("expert", None),
        P("expert", "dp", None),
        P("expert", "dp", None),
        P("expert", None, "dp"),
    )
    out_specs = (
        P("expert", "dp"),
        P("expert", "dp"),
        P("expert", "dp", None),
        P("expert", "dp", None),
        P("expert", None, "dp"),
    )
    return jax.shard_map(local, mesh=mesh, in_specs=in_specs, out_specs=out_specs, check_vma=False)
```

```python
import jax
import jax.numpy as jnp
from jax import lax
from jax.sharding import PartitionSpec as P


def swiglu_parts(gate_sum, up_sum, back_sum):
    logistic = jax.nn.sigmoid(gate_sum)
    activated = gate_sum * logistic
    hidden = (activated * up_sum).astype(jnp.bfloat16)
    gate_delta = (back_sum * up_sum * logistic * (1.0 + gate_sum * (1.0 - logistic))).astype(
        jnp.bfloat16
    )
    up_delta = (back_sum * activated).astype(jnp.bfloat16)
    return (hidden, gate_delta, up_delta)


def split_f32(value):
    high = value.astype(jnp.bfloat16)
    rest = value - high.astype(jnp.float32)
    middle = rest.astype(jnp.bfloat16)
    low = (rest - middle.astype(jnp.float32)).astype(jnp.bfloat16)
    return high, middle, low


def local(tokens, out_grad, expert_ids, route_weights, gate_weight, up_weight, down_weight):
    token_count, width_dev = tokens.shape
    per_token = expert_ids.shape[1]
    local_experts = gate_weight.shape[0]
    hidden_units = gate_weight.shape[2]
    sources = lax.axis_size("expert")
    experts = local_experts * sources
    capacity = 2 * token_count * per_token // experts
    slot_count = token_count * per_token
    me = lax.axis_index("expert")

    high, middle, low = split_f32(route_weights)
    route_cols = 4 * per_token
    pad_cols = (-route_cols) % 128
    packed = jnp.concatenate(
        [
            tokens,
            out_grad,
            expert_ids.astype(jnp.bfloat16),
            high,
            middle,
            low,
            jnp.zeros((token_count, pad_cols), jnp.bfloat16),
        ],
        axis=1,
    )
    gathered = lax.all_gather(packed, "expert", axis=0, tiled=True)
    feats = gathered[:, : 2 * width_dev]
    route_all = gathered[:, 2 * width_dev : 2 * width_dev + route_cols].astype(jnp.float32)
    ids_all = route_all[:, :per_token].astype(jnp.int32)
    w_all = (
        route_all[:, per_token : 2 * per_token] + route_all[:, 2 * per_token : 3 * per_token]
    ) + route_all[:, 3 * per_token :]
    all_tokens = sources * token_count

    flat_all = ids_all.reshape(sources, slot_count)
    position = jnp.arange(slot_count, dtype=jnp.int32)
    earlier = (flat_all[:, None, :] == flat_all[:, :, None]) & (
        position[None, None, :] < position[None, :, None]
    )
    rank_all = jnp.sum(earlier.astype(jnp.int32), axis=2)
    local_e = flat_all - me * local_experts
    is_local = (local_e >= 0) & (local_e < local_experts)
    src = jnp.arange(sources, dtype=jnp.int32)[:, None]
    row_count = local_experts * sources * capacity
    row_of = jnp.where(is_local, (local_e * sources + src) * capacity + rank_all, row_count)
    row_of = row_of.reshape(sources * slot_count)
    token_of = jnp.arange(sources * slot_count, dtype=jnp.int32) // per_token
    target = jnp.arange(row_count, dtype=jnp.int32)
    hit = target[:, None] == row_of[None, :]
    holder = jnp.sum(jnp.where(hit, token_of[None, :] + 1, 0), axis=1) - 1
    row_weight = jnp.sum(jnp.where(hit, w_all.reshape(-1)[None, :], 0.0), axis=1)
    select = (holder[:, None] == jnp.arange(all_tokens, dtype=jnp.int32)[None, :]).astype(
        jnp.bfloat16
    )
    picked = jnp.dot(select, feats, preferred_element_type=jnp.float32)
    x_in = picked[:, :width_dev].astype(jnp.bfloat16)
    dy_in = (row_weight[:, None] * picked[:, width_dev:]).astype(jnp.bfloat16)
    x_in = x_in.reshape(local_experts, sources * capacity, width_dev)
    dy_in = dy_in.reshape(local_experts, sources * capacity, width_dev)

    gate_part = jnp.einsum(
        "jrd,jdf->jrf", x_in, gate_weight, preferred_element_type=jnp.float32
    ).astype(jnp.bfloat16)
    up_part = jnp.einsum(
        "jrd,jdf->jrf", x_in, up_weight, preferred_element_type=jnp.float32
    ).astype(jnp.bfloat16)
    front = jnp.concatenate([gate_part, up_part], axis=2).reshape(row_count, 2 * hidden_units)
    front_sums = lax.psum_scatter(front, "dp", scatter_dimension=0, tiled=True)
    back_part = jnp.einsum(
        "jrd,jfd->jrf", dy_in, down_weight, preferred_element_type=jnp.float32
    ).astype(jnp.bfloat16)
    back_sums = lax.psum_scatter(
        back_part.reshape(row_count, hidden_units), "dp", scatter_dimension=0, tiled=True
    )
    front_sums = front_sums.astype(jnp.float32)
    hidden, gate_delta, up_delta = swiglu_parts(
        front_sums[:, :hidden_units], front_sums[:, hidden_units:], back_sums.astype(jnp.float32)
    )
    hidden = lax.all_gather(hidden, "dp", axis=0, tiled=True)
    deltas = lax.all_gather(
        jnp.concatenate([gate_delta, up_delta], axis=1), "dp", axis=0, tiled=True
    )
    expert_shape = (local_experts, sources, capacity, hidden_units)
    hidden = hidden.reshape(expert_shape)
    gate_delta = deltas[:, :hidden_units].reshape(expert_shape)
    up_delta = deltas[:, hidden_units:].reshape(expert_shape)
    in_tokens = x_in.reshape(local_experts, sources, capacity, width_dev)
    in_grads = dy_in.reshape(local_experts, sources, capacity, width_dev)

    buffer_rows = experts * capacity
    expert_out = jnp.einsum(
        "jscf,jfd->sjcd", hidden, down_weight, preferred_element_type=jnp.float32
    ).astype(jnp.bfloat16)
    out_back = lax.all_to_all(
        expert_out.reshape(buffer_rows, width_dev), "expert", split_axis=0, concat_axis=0, tiled=True
    )
    down_grad = jnp.einsum(
        "jscf,jscd->jfd", hidden, in_grads, preferred_element_type=jnp.float32
    ).astype(jnp.bfloat16)
    expert_back = (
        jnp.einsum("jscf,jdf->sjcd", gate_delta, gate_weight, preferred_element_type=jnp.float32)
        + jnp.einsum("jscf,jdf->sjcd", up_delta, up_weight, preferred_element_type=jnp.float32)
    ).astype(jnp.bfloat16)
    grad_back = lax.all_to_all(
        expert_back.reshape(buffer_rows, width_dev), "expert", split_axis=0, concat_axis=0, tiled=True
    )
    gate_grad = jnp.einsum(
        "jscd,jscf->jdf", in_tokens, gate_delta, preferred_element_type=jnp.float32
    ).astype(jnp.bfloat16)
    up_grad = jnp.einsum(
        "jscd,jscf->jdf", in_tokens, up_delta, preferred_element_type=jnp.float32
    ).astype(jnp.bfloat16)

    flat_ids = expert_ids.reshape(slot_count)
    earlier_local = (flat_ids[None, :] == flat_ids[:, None]) & (
        position[None, :] < position[:, None]
    )
    slot_rank = jnp.sum(earlier_local.astype(jnp.int32), axis=1)
    slot_place = (flat_ids * capacity + slot_rank).reshape(token_count, per_token)
    picked_out = jnp.take(out_back, slot_place, axis=0).astype(jnp.float32)
    layer_out = jnp.sum(picked_out * route_weights[:, :, None], axis=1).astype(jnp.bfloat16)
    picked_back = jnp.take(grad_back, slot_place, axis=0).astype(jnp.float32)
    grad_tokens = jnp.sum(picked_back, axis=1).astype(jnp.bfloat16)
    return (layer_out, grad_tokens, gate_grad, up_grad, down_grad)


def solution(mesh):
    in_specs = (
        P("expert", "dp"),
        P("expert", "dp"),
        P("expert", None),
        P("expert", None),
        P("expert", "dp", None),
        P("expert", "dp", None),
        P("expert", None, "dp"),
    )
    out_specs = (
        P("expert", "dp"),
        P("expert", "dp"),
        P("expert", "dp", None),
        P("expert", "dp", None),
        P("expert", None, "dp"),
    )
    return jax.shard_map(local, mesh=mesh, in_specs=in_specs, out_specs=out_specs, check_vma=False)
```

```python
import jax
import jax.numpy as jnp
from jax import lax
from jax.sharding import PartitionSpec as P


def swiglu_parts(gate_sum, up_sum, back_sum):
    logistic = jax.nn.sigmoid(gate_sum)
    activated = gate_sum * logistic
    hidden = (activated * up_sum).astype(jnp.bfloat16)
    gate_delta = (back_sum * up_sum * logistic * (1.0 + gate_sum * (1.0 - logistic))).astype(
        jnp.bfloat16
    )
    up_delta = (back_sum * activated).astype(jnp.bfloat16)
    return (hidden, gate_delta, up_delta)


def split_f32(value):
    high = value.astype(jnp.bfloat16)
    rest = value - high.astype(jnp.float32)
    middle = rest.astype(jnp.bfloat16)
    low = (rest - middle.astype(jnp.float32)).astype(jnp.bfloat16)
    return high, middle, low


def local(tokens, out_grad, expert_ids, route_weights, gate_weight, up_weight, down_weight):
    token_count, width_dev = tokens.shape
    per_token = expert_ids.shape[1]
    local_experts = gate_weight.shape[0]
    hidden_units = gate_weight.shape[2]
    sources = lax.axis_size("expert")
    experts = local_experts * sources
    capacity = 2 * token_count * per_token // experts
    slot_count = token_count * per_token
    me = lax.axis_index("expert")

    high, middle, low = split_f32(route_weights)
    route_cols = 4 * per_token
    pad_cols = (-route_cols) % 128
    packed = jnp.concatenate(
        [
            tokens,
            out_grad,
            expert_ids.astype(jnp.bfloat16),
            high,
            middle,
            low,
            jnp.zeros((token_count, pad_cols), jnp.bfloat16),
        ],
        axis=1,
    )
    gathered = lax.all_gather(packed, "expert", axis=0, tiled=True)
    feats = gathered[:, : 2 * width_dev]
    route_all = gathered[:, 2 * width_dev : 2 * width_dev + route_cols].astype(jnp.float32)
    ids_all = route_all[:, :per_token].astype(jnp.int32)
    w_all = (
        route_all[:, per_token : 2 * per_token] + route_all[:, 2 * per_token : 3 * per_token]
    ) + route_all[:, 3 * per_token :]
    all_tokens = sources * token_count

    flat_all = ids_all.reshape(sources, slot_count)
    position = jnp.arange(slot_count, dtype=jnp.int32)
    earlier = (flat_all[:, None, :] == flat_all[:, :, None]) & (
        position[None, None, :] < position[None, :, None]
    )
    rank_all = jnp.sum(earlier.astype(jnp.int32), axis=2)
    local_e = flat_all - me * local_experts
    is_local = (local_e >= 0) & (local_e < local_experts)
    src = jnp.arange(sources, dtype=jnp.int32)[:, None]
    row_count = local_experts * sources * capacity
    row_of = jnp.where(is_local, (local_e * sources + src) * capacity + rank_all, row_count)
    row_of = row_of.reshape(sources * slot_count)
    token_of = jnp.arange(sources * slot_count, dtype=jnp.int32) // per_token
    target = jnp.arange(row_count, dtype=jnp.int32)
    hit = target[:, None] == row_of[None, :]
    holder = jnp.sum(jnp.where(hit, token_of[None, :] + 1, 0), axis=1) - 1
    row_weight = jnp.sum(jnp.where(hit, w_all.reshape(-1)[None, :], 0.0), axis=1)
    select = (holder[:, None] == jnp.arange(all_tokens, dtype=jnp.int32)[None, :]).astype(
        jnp.bfloat16
    )
    picked = jnp.dot(select, feats, preferred_element_type=jnp.float32)
    x_in = picked[:, :width_dev].astype(jnp.bfloat16)
    dy_in = (row_weight[:, None] * picked[:, width_dev:]).astype(jnp.bfloat16)
    x_in = x_in.reshape(local_experts, sources * capacity, width_dev)
    dy_in = dy_in.reshape(local_experts, sources * capacity, width_dev)

    gate_part = jnp.einsum(
        "jrd,jdf->jrf", x_in, gate_weight, preferred_element_type=jnp.float32
    ).astype(jnp.bfloat16)
    up_part = jnp.einsum(
        "jrd,jdf->jrf", x_in, up_weight, preferred_element_type=jnp.float32
    ).astype(jnp.bfloat16)
    front = jnp.concatenate([gate_part, up_part], axis=2).reshape(row_count, 2 * hidden_units)
    front_sums = lax.psum_scatter(front, "dp", scatter_dimension=0, tiled=True)
    back_part = jnp.einsum(
        "jrd,jfd->jrf", dy_in, down_weight, preferred_element_type=jnp.float32
    ).astype(jnp.bfloat16)
    back_sums = lax.psum_scatter(
        back_part.reshape(row_count, hidden_units), "dp", scatter_dimension=0, tiled=True
    )
    front_sums = front_sums.astype(jnp.float32)
    hidden, gate_delta, up_delta = swiglu_parts(
        front_sums[:, :hidden_units], front_sums[:, hidden_units:], back_sums.astype(jnp.float32)
    )
    expert_shape = (local_experts, sources, capacity, hidden_units)
    hidden = lax.all_gather(hidden, "dp", axis=0, tiled=True).reshape(expert_shape)
    gate_delta = lax.all_gather(gate_delta, "dp", axis=0, tiled=True).reshape(expert_shape)
    up_delta = lax.all_gather(up_delta, "dp", axis=0, tiled=True).reshape(expert_shape)
    in_tokens = x_in.reshape(local_experts, sources, capacity, width_dev)
    in_grads = dy_in.reshape(local_experts, sources, capacity, width_dev)

    buffer_rows = experts * capacity
    expert_out = jnp.einsum(
        "jscf,jfd->sjcd", hidden, down_weight, preferred_element_type=jnp.float32
    ).astype(jnp.bfloat16)
    out_back = lax.all_to_all(
        expert_out.reshape(buffer_rows, width_dev), "expert", split_axis=0, concat_axis=0, tiled=True
    )
    down_grad = jnp.einsum(
        "jscf,jscd->jfd", hidden, in_grads, preferred_element_type=jnp.float32
    ).astype(jnp.bfloat16)
    gate_grad = jnp.einsum(
        "jscd,jscf->jdf", in_tokens, gate_delta, preferred_element_type=jnp.float32
    ).astype(jnp.bfloat16)
    expert_back = (
        jnp.einsum("jscf,jdf->sjcd", gate_delta, gate_weight, preferred_element_type=jnp.float32)
        + jnp.einsum("jscf,jdf->sjcd", up_delta, up_weight, preferred_element_type=jnp.float32)
    ).astype(jnp.bfloat16)
    grad_back = lax.all_to_all(
        expert_back.reshape(buffer_rows, width_dev), "expert", split_axis=0, concat_axis=0, tiled=True
    )
    up_grad = jnp.einsum(
        "jscd,jscf->jdf", in_tokens, up_delta, preferred_element_type=jnp.float32
    ).astype(jnp.bfloat16)

    flat_ids = expert_ids.reshape(slot_count)
    earlier_local = (flat_ids[None, :] == flat_ids[:, None]) & (
        position[None, :] < position[:, None]
    )
    slot_rank = jnp.sum(earlier_local.astype(jnp.int32), axis=1)
    slot_place = (flat_ids * capacity + slot_rank).reshape(token_count, per_token)
    picked_out = jnp.take(out_back, slot_place, axis=0).astype(jnp.float32)
    layer_out = jnp.sum(picked_out * route_weights[:, :, None], axis=1).astype(jnp.bfloat16)
    picked_back = jnp.take(grad_back, slot_place, axis=0).astype(jnp.float32)
    grad_tokens = jnp.sum(picked_back, axis=1).astype(jnp.bfloat16)
    return (layer_out, grad_tokens, gate_grad, up_grad, down_grad)


def solution(mesh):
    in_specs = (
        P("expert", "dp"),
        P("expert", "dp"),
        P("expert", None),
        P("expert", None),
        P("expert", "dp", None),
        P("expert", "dp", None),
        P("expert", None, "dp"),
    )
    out_specs = (
        P("expert", "dp"),
        P("expert", "dp"),
        P("expert", "dp", None),
        P("expert", "dp", None),
        P("expert", None, "dp"),
    )
    return jax.shard_map(local, mesh=mesh, in_specs=in_specs, out_specs=out_specs, check_vma=False)
```

```python
import jax
import jax.numpy as jnp
from jax import lax
from jax.sharding import PartitionSpec as P


def swiglu_parts(gate_sum, up_sum, back_sum):
    logistic = jax.nn.sigmoid(gate_sum)
    activated = gate_sum * logistic
    hidden = (activated * up_sum).astype(jnp.bfloat16)
    gate_delta = (back_sum * up_sum * logistic * (1.0 + gate_sum * (1.0 - logistic))).astype(
        jnp.bfloat16
    )
    up_delta = (back_sum * activated).astype(jnp.bfloat16)
    return (hidden, gate_delta, up_delta)


def split_f32(value):
    high = value.astype(jnp.bfloat16)
    rest = value - high.astype(jnp.float32)
    middle = rest.astype(jnp.bfloat16)
    low = (rest - middle.astype(jnp.float32)).astype(jnp.bfloat16)
    return high, middle, low


def local(tokens, out_grad, expert_ids, route_weights, gate_weight, up_weight, down_weight):
    token_count, width_dev = tokens.shape
    per_token = expert_ids.shape[1]
    local_experts = gate_weight.shape[0]
    hidden_units = gate_weight.shape[2]
    sources = lax.axis_size("expert")
    experts = local_experts * sources
    capacity = 2 * token_count * per_token // experts
    slot_count = token_count * per_token
    me = lax.axis_index("expert")

    high, middle, low = split_f32(route_weights)
    route_cols = 4 * per_token
    pad_cols = (-route_cols) % 128
    packed = jnp.concatenate(
        [
            tokens,
            out_grad,
            expert_ids.astype(jnp.bfloat16),
            high,
            middle,
            low,
            jnp.zeros((token_count, pad_cols), jnp.bfloat16),
        ],
        axis=1,
    )
    gathered = lax.all_gather(packed, "expert", axis=0, tiled=True)
    feats = gathered[:, : 2 * width_dev]
    route_all = gathered[:, 2 * width_dev : 2 * width_dev + route_cols].astype(jnp.float32)
    ids_all = route_all[:, :per_token].astype(jnp.int32)
    w_all = (
        route_all[:, per_token : 2 * per_token] + route_all[:, 2 * per_token : 3 * per_token]
    ) + route_all[:, 3 * per_token :]
    all_tokens = sources * token_count

    flat_all = ids_all.reshape(sources, slot_count)
    position = jnp.arange(slot_count, dtype=jnp.int32)
    earlier = (flat_all[:, None, :] == flat_all[:, :, None]) & (
        position[None, None, :] < position[None, :, None]
    )
    rank_all = jnp.sum(earlier.astype(jnp.int32), axis=2)
    local_e = flat_all - me * local_experts
    is_local = (local_e >= 0) & (local_e < local_experts)
    src = jnp.arange(sources, dtype=jnp.int32)[:, None]
    row_count = local_experts * sources * capacity
    row_of = jnp.where(is_local, (local_e * sources + src) * capacity + rank_all, row_count)
    row_of = row_of.reshape(sources * slot_count)
    token_of = jnp.arange(sources * slot_count, dtype=jnp.int32) // per_token
    target = jnp.arange(row_count, dtype=jnp.int32)
    hit = target[:, None] == row_of[None, :]
    holder = jnp.sum(jnp.where(hit, token_of[None, :] + 1, 0), axis=1) - 1
    row_weight = jnp.sum(jnp.where(hit, w_all.reshape(-1)[None, :], 0.0), axis=1)
    select = (holder[:, None] == jnp.arange(all_tokens, dtype=jnp.int32)[None, :]).astype(
        jnp.bfloat16
    )
    picked = jnp.dot(select, feats, preferred_element_type=jnp.float32)
    x_in = picked[:, :width_dev].astype(jnp.bfloat16)
    dy_in = (row_weight[:, None] * picked[:, width_dev:]).astype(jnp.bfloat16)
    x_in = x_in.reshape(local_experts, sources * capacity, width_dev)
    dy_in = dy_in.reshape(local_experts, sources * capacity, width_dev)

    gate_part = jnp.einsum(
        "jrd,jdf->jrf", x_in, gate_weight, preferred_element_type=jnp.float32
    ).astype(jnp.bfloat16)
    up_part = jnp.einsum(
        "jrd,jdf->jrf", x_in, up_weight, preferred_element_type=jnp.float32
    ).astype(jnp.bfloat16)
    front = jnp.concatenate([gate_part, up_part], axis=2).reshape(row_count, 2 * hidden_units)
    front_sums = lax.psum_scatter(front, "dp", scatter_dimension=0, tiled=True)
    back_part = jnp.einsum(
        "jrd,jfd->jrf", dy_in, down_weight, preferred_element_type=jnp.float32
    ).astype(jnp.bfloat16)
    back_sums = lax.psum_scatter(
        back_part.reshape(row_count, hidden_units), "dp", scatter_dimension=0, tiled=True
    )
    front_sums = front_sums.astype(jnp.float32)
    hidden, gate_delta, up_delta = swiglu_parts(
        front_sums[:, :hidden_units], front_sums[:, hidden_units:], back_sums.astype(jnp.float32)
    )
    deltas = lax.all_gather(
        jnp.concatenate([gate_delta, up_delta], axis=1), "dp", axis=0, tiled=True
    )
    hidden, deltas = lax.optimization_barrier((hidden, deltas))
    hidden = lax.all_gather(hidden, "dp", axis=0, tiled=True)
    expert_shape = (local_experts, sources, capacity, hidden_units)
    hidden = hidden.reshape(expert_shape)
    gate_delta = deltas[:, :hidden_units].reshape(expert_shape)
    up_delta = deltas[:, hidden_units:].reshape(expert_shape)
    in_tokens = x_in.reshape(local_experts, sources, capacity, width_dev)
    in_grads = dy_in.reshape(local_experts, sources, capacity, width_dev)

    buffer_rows = experts * capacity
    expert_out = jnp.einsum(
        "jscf,jfd->sjcd", hidden, down_weight, preferred_element_type=jnp.float32
    ).astype(jnp.bfloat16)
    out_back = lax.all_to_all(
        expert_out.reshape(buffer_rows, width_dev), "expert", split_axis=0, concat_axis=0, tiled=True
    )
    down_grad = jnp.einsum(
        "jscf,jscd->jfd", hidden, in_grads, preferred_element_type=jnp.float32
    ).astype(jnp.bfloat16)
    expert_back = (
        jnp.einsum("jscf,jdf->sjcd", gate_delta, gate_weight, preferred_element_type=jnp.float32)
        + jnp.einsum("jscf,jdf->sjcd", up_delta, up_weight, preferred_element_type=jnp.float32)
    ).astype(jnp.bfloat16)
    grad_back = lax.all_to_all(
        expert_back.reshape(buffer_rows, width_dev), "expert", split_axis=0, concat_axis=0, tiled=True
    )
    gate_grad = jnp.einsum(
        "jscd,jscf->jdf", in_tokens, gate_delta, preferred_element_type=jnp.float32
    ).astype(jnp.bfloat16)
    up_grad = jnp.einsum(
        "jscd,jscf->jdf", in_tokens, up_delta, preferred_element_type=jnp.float32
    ).astype(jnp.bfloat16)

    flat_ids = expert_ids.reshape(slot_count)
    earlier_local = (flat_ids[None, :] == flat_ids[:, None]) & (
        position[None, :] < position[:, None]
    )
    slot_rank = jnp.sum(earlier_local.astype(jnp.int32), axis=1)
    slot_place = (flat_ids * capacity + slot_rank).reshape(token_count, per_token)
    picked_out = jnp.take(out_back, slot_place, axis=0).astype(jnp.float32)
    layer_out = jnp.sum(picked_out * route_weights[:, :, None], axis=1).astype(jnp.bfloat16)
    picked_back = jnp.take(grad_back, slot_place, axis=0).astype(jnp.float32)
    grad_tokens = jnp.sum(picked_back, axis=1).astype(jnp.bfloat16)
    return (layer_out, grad_tokens, gate_grad, up_grad, down_grad)


def solution(mesh):
    in_specs = (
        P("expert", "dp"),
        P("expert", "dp"),
        P("expert", None),
        P("expert", None),
        P("expert", "dp", None),
        P("expert", "dp", None),
        P("expert", None, "dp"),
    )
    out_specs = (
        P("expert", "dp"),
        P("expert", "dp"),
        P("expert", "dp", None),
        P("expert", "dp", None),
        P("expert", None, "dp"),
    )
    return jax.shard_map(local, mesh=mesh, in_specs=in_specs, out_specs=out_specs, check_vma=False)
```

```python
import jax
import jax.numpy as jnp
from jax import lax
from jax.sharding import PartitionSpec as P


def swiglu_parts(gate_sum, up_sum, back_sum):
    logistic = jax.nn.sigmoid(gate_sum)
    activated = gate_sum * logistic
    hidden = (activated * up_sum).astype(jnp.bfloat16)
    gate_delta = (back_sum * up_sum * logistic * (1.0 + gate_sum * (1.0 - logistic))).astype(
        jnp.bfloat16
    )
    up_delta = (back_sum * activated).astype(jnp.bfloat16)
    return (hidden, gate_delta, up_delta)


def split_f32(value):
    high = value.astype(jnp.bfloat16)
    rest = value - high.astype(jnp.float32)
    middle = rest.astype(jnp.bfloat16)
    low = (rest - middle.astype(jnp.float32)).astype(jnp.bfloat16)
    return high, middle, low


def local(tokens, out_grad, expert_ids, route_weights, gate_weight, up_weight, down_weight):
    token_count, width_dev = tokens.shape
    per_token = expert_ids.shape[1]
    local_experts = gate_weight.shape[0]
    hidden_units = gate_weight.shape[2]
    sources = lax.axis_size("expert")
    experts = local_experts * sources
    capacity = 2 * token_count * per_token // experts
    slot_count = token_count * per_token
    me = lax.axis_index("expert")

    high, middle, low = split_f32(route_weights)
    route_cols = 4 * per_token
    pad_cols = (-route_cols) % 128
    packed = jnp.concatenate(
        [
            tokens,
            out_grad,
            expert_ids.astype(jnp.bfloat16),
            high,
            middle,
            low,
            jnp.zeros((token_count, pad_cols), jnp.bfloat16),
        ],
        axis=1,
    )
    gathered = lax.all_gather(packed, "expert", axis=0, tiled=True)
    feats = gathered[:, : 2 * width_dev]
    route_all = gathered[:, 2 * width_dev : 2 * width_dev + route_cols].astype(jnp.float32)
    ids_all = route_all[:, :per_token].astype(jnp.int32)
    w_all = (
        route_all[:, per_token : 2 * per_token] + route_all[:, 2 * per_token : 3 * per_token]
    ) + route_all[:, 3 * per_token :]
    all_tokens = sources * token_count

    flat_all = ids_all.reshape(sources, slot_count)
    position = jnp.arange(slot_count, dtype=jnp.int32)
    earlier = (flat_all[:, None, :] == flat_all[:, :, None]) & (
        position[None, None, :] < position[None, :, None]
    )
    rank_all = jnp.sum(earlier.astype(jnp.int32), axis=2)
    local_e = flat_all - me * local_experts
    is_local = (local_e >= 0) & (local_e < local_experts)
    src = jnp.arange(sources, dtype=jnp.int32)[:, None]
    row_count = local_experts * sources * capacity
    row_of = jnp.where(is_local, (local_e * sources + src) * capacity + rank_all, row_count)
    row_of = row_of.reshape(sources * slot_count)
    token_of = jnp.arange(sources * slot_count, dtype=jnp.int32) // per_token
    target = jnp.arange(row_count, dtype=jnp.int32)
    hit = target[:, None] == row_of[None, :]
    holder = jnp.sum(jnp.where(hit, token_of[None, :] + 1, 0), axis=1) - 1
    row_weight = jnp.sum(jnp.where(hit, w_all.reshape(-1)[None, :], 0.0), axis=1)
    select = (holder[:, None] == jnp.arange(all_tokens, dtype=jnp.int32)[None, :]).astype(
        jnp.bfloat16
    )
    picked = jnp.dot(select, feats, preferred_element_type=jnp.float32)
    x_in = picked[:, :width_dev].astype(jnp.bfloat16)
    dy_in = (row_weight[:, None] * picked[:, width_dev:]).astype(jnp.bfloat16)
    x_in = x_in.reshape(local_experts, sources * capacity, width_dev)
    dy_in = dy_in.reshape(local_experts, sources * capacity, width_dev)

    gate_part = jnp.einsum(
        "jrd,jdf->jrf", x_in, gate_weight, preferred_element_type=jnp.float32
    ).astype(jnp.bfloat16)
    up_part = jnp.einsum(
        "jrd,jdf->jrf", x_in, up_weight, preferred_element_type=jnp.float32
    ).astype(jnp.bfloat16)
    front = jnp.concatenate([gate_part, up_part], axis=2).reshape(row_count, 2 * hidden_units)
    front_sums = lax.psum_scatter(front, "dp", scatter_dimension=0, tiled=True)
    back_part = jnp.einsum(
        "jrd,jfd->jrf", dy_in, down_weight, preferred_element_type=jnp.float32
    ).astype(jnp.bfloat16)
    back_sums = lax.psum_scatter(
        back_part.reshape(row_count, hidden_units), "dp", scatter_dimension=0, tiled=True
    )
    front_sums = front_sums.astype(jnp.float32)
    hidden, gate_delta, up_delta = swiglu_parts(
        front_sums[:, :hidden_units], front_sums[:, hidden_units:], back_sums.astype(jnp.float32)
    )
    first = lax.all_gather(
        jnp.concatenate([hidden, gate_delta], axis=1), "dp", axis=0, tiled=True
    )
    up_delta, first = lax.optimization_barrier((up_delta, first))
    up_delta = lax.all_gather(up_delta, "dp", axis=0, tiled=True)
    rows_shape = (local_experts, sources * capacity, hidden_units)
    expert_shape = (local_experts, sources, capacity, hidden_units)
    hidden = first[:, :hidden_units]
    gate_delta = first[:, hidden_units:]

    buffer_rows = experts * capacity
    expert_out = jnp.einsum(
        "jscf,jfd->sjcd", hidden.reshape(expert_shape), down_weight,
        preferred_element_type=jnp.float32,
    ).astype(jnp.bfloat16)
    out_back = lax.all_to_all(
        expert_out.reshape(buffer_rows, width_dev), "expert", split_axis=0, concat_axis=0, tiled=True
    )
    down_grad = jnp.einsum(
        "jrf,jrd->jfd", hidden.reshape(rows_shape), dy_in, preferred_element_type=jnp.float32
    ).astype(jnp.bfloat16)
    gate_back = jnp.einsum(
        "jscf,jdf->sjcd", gate_delta.reshape(expert_shape), gate_weight,
        preferred_element_type=jnp.float32,
    )
    gate_grad = jnp.einsum(
        "jrd,jrf->jdf", x_in, gate_delta.reshape(rows_shape), preferred_element_type=jnp.float32
    ).astype(jnp.bfloat16)
    expert_back = (
        gate_back
        + jnp.einsum(
            "jscf,jdf->sjcd", up_delta.reshape(expert_shape), up_weight,
            preferred_element_type=jnp.float32,
        )
    ).astype(jnp.bfloat16)
    grad_back = lax.all_to_all(
        expert_back.reshape(buffer_rows, width_dev), "expert", split_axis=0, concat_axis=0, tiled=True
    )
    up_grad = jnp.einsum(
        "jrd,jrf->jdf", x_in, up_delta.reshape(rows_shape), preferred_element_type=jnp.float32
    ).astype(jnp.bfloat16)

    flat_ids = expert_ids.reshape(slot_count)
    earlier_local = (flat_ids[None, :] == flat_ids[:, None]) & (
        position[None, :] < position[:, None]
    )
    slot_rank = jnp.sum(earlier_local.astype(jnp.int32), axis=1)
    slot_place = (flat_ids * capacity + slot_rank).reshape(token_count, per_token)
    picked_out = jnp.take(out_back, slot_place, axis=0).astype(jnp.float32)
    layer_out = jnp.sum(picked_out * route_weights[:, :, None], axis=1).astype(jnp.bfloat16)
    picked_back = jnp.take(grad_back, slot_place, axis=0).astype(jnp.float32)
    grad_tokens = jnp.sum(picked_back, axis=1).astype(jnp.bfloat16)
    return (layer_out, grad_tokens, gate_grad, up_grad, down_grad)


def solution(mesh):
    in_specs = (
        P("expert", "dp"),
        P("expert", "dp"),
        P("expert", None),
        P("expert", None),
        P("expert", "dp", None),
        P("expert", "dp", None),
        P("expert", None, "dp"),
    )
    out_specs = (
        P("expert", "dp"),
        P("expert", "dp"),
        P("expert", "dp", None),
        P("expert", "dp", None),
        P("expert", None, "dp"),
    )
    return jax.shard_map(local, mesh=mesh, in_specs=in_specs, out_specs=out_specs, check_vma=False)
```

```python
import jax
import jax.numpy as jnp
from jax import lax
from jax.sharding import PartitionSpec as P


def swiglu_parts(gate_sum, up_sum, back_sum):
    logistic = jax.nn.sigmoid(gate_sum)
    activated = gate_sum * logistic
    hidden = (activated * up_sum).astype(jnp.bfloat16)
    gate_delta = (back_sum * up_sum * logistic * (1.0 + gate_sum * (1.0 - logistic))).astype(
        jnp.bfloat16
    )
    up_delta = (back_sum * activated).astype(jnp.bfloat16)
    return (hidden, gate_delta, up_delta)


def split_f32(value):
    high = value.astype(jnp.bfloat16)
    rest = value - high.astype(jnp.float32)
    middle = rest.astype(jnp.bfloat16)
    low = (rest - middle.astype(jnp.float32)).astype(jnp.bfloat16)
    return high, middle, low


def local(tokens, out_grad, expert_ids, route_weights, gate_weight, up_weight, down_weight):
    token_count, width_dev = tokens.shape
    per_token = expert_ids.shape[1]
    local_experts = gate_weight.shape[0]
    hidden_units = gate_weight.shape[2]
    sources = lax.axis_size("expert")
    experts = local_experts * sources
    capacity = 2 * token_count * per_token // experts
    slot_count = token_count * per_token
    me = lax.axis_index("expert")

    high, middle, low = split_f32(route_weights)
    route_cols = 4 * per_token
    pad_cols = (-route_cols) % 128
    packed = jnp.concatenate(
        [
            tokens,
            out_grad,
            expert_ids.astype(jnp.bfloat16),
            high,
            middle,
            low,
            jnp.zeros((token_count, pad_cols), jnp.bfloat16),
        ],
        axis=1,
    )
    gathered = lax.all_gather(packed, "expert", axis=0, tiled=True)
    feats = gathered[:, : 2 * width_dev]
    route_all = gathered[:, 2 * width_dev : 2 * width_dev + route_cols].astype(jnp.float32)
    ids_all = route_all[:, :per_token].astype(jnp.int32)
    w_all = (
        route_all[:, per_token : 2 * per_token] + route_all[:, 2 * per_token : 3 * per_token]
    ) + route_all[:, 3 * per_token :]
    all_tokens = sources * token_count

    flat_all = ids_all.reshape(sources, slot_count)
    position = jnp.arange(slot_count, dtype=jnp.int32)
    earlier = (flat_all[:, None, :] == flat_all[:, :, None]) & (
        position[None, None, :] < position[None, :, None]
    )
    rank_all = jnp.sum(earlier.astype(jnp.int32), axis=2)
    local_e = flat_all - me * local_experts
    is_local = (local_e >= 0) & (local_e < local_experts)
    src = jnp.arange(sources, dtype=jnp.int32)[:, None]
    row_count = local_experts * sources * capacity
    row_of = jnp.where(is_local, (local_e * sources + src) * capacity + rank_all, row_count)
    row_of = row_of.reshape(sources * slot_count)
    token_of = jnp.arange(sources * slot_count, dtype=jnp.int32) // per_token
    target = jnp.arange(row_count, dtype=jnp.int32)
    hit = target[:, None] == row_of[None, :]
    holder = jnp.sum(jnp.where(hit, token_of[None, :] + 1, 0), axis=1) - 1
    row_weight = jnp.sum(jnp.where(hit, w_all.reshape(-1)[None, :], 0.0), axis=1)
    select = (holder[:, None] == jnp.arange(all_tokens, dtype=jnp.int32)[None, :]).astype(
        jnp.bfloat16
    )
    picked = jnp.dot(select, feats, preferred_element_type=jnp.float32)
    x_in = picked[:, :width_dev].astype(jnp.bfloat16)
    dy_in = (row_weight[:, None] * picked[:, width_dev:]).astype(jnp.bfloat16)
    x_in = x_in.reshape(local_experts, sources * capacity, width_dev)
    dy_in = dy_in.reshape(local_experts, sources * capacity, width_dev)

    gate_part = jnp.einsum(
        "jrd,jdf->jrf", x_in, gate_weight, preferred_element_type=jnp.float32
    ).astype(jnp.bfloat16)
    up_part = jnp.einsum(
        "jrd,jdf->jrf", x_in, up_weight, preferred_element_type=jnp.float32
    ).astype(jnp.bfloat16)
    front = jnp.concatenate([gate_part, up_part], axis=2).reshape(row_count, 2 * hidden_units)
    front_sums = lax.psum_scatter(front, "dp", scatter_dimension=0, tiled=True)
    back_part = jnp.einsum(
        "jrd,jfd->jrf", dy_in, down_weight, preferred_element_type=jnp.float32
    ).astype(jnp.bfloat16)
    back_sums = lax.psum_scatter(
        back_part.reshape(row_count, hidden_units), "dp", scatter_dimension=0, tiled=True
    )
    front_sums = front_sums.astype(jnp.float32)
    hidden, gate_delta, up_delta = swiglu_parts(
        front_sums[:, :hidden_units], front_sums[:, hidden_units:], back_sums.astype(jnp.float32)
    )
    hidden = lax.all_gather(hidden, "dp", axis=0, tiled=True)
    deltas = lax.all_gather(
        jnp.concatenate([gate_delta, up_delta], axis=1), "dp", axis=0, tiled=True
    )
    expert_shape = (local_experts, sources, capacity, hidden_units)
    hidden = hidden.reshape(expert_shape)
    gate_delta = deltas[:, :hidden_units].reshape(expert_shape)
    up_delta = deltas[:, hidden_units:].reshape(expert_shape)
    rows_shape = (local_experts, sources * capacity, hidden_units)

    buffer_rows = experts * capacity
    expert_out = jnp.einsum(
        "jscf,jfd->sjcd", hidden, down_weight, preferred_element_type=jnp.float32
    ).astype(jnp.bfloat16)
    out_back = lax.all_to_all(
        expert_out.reshape(buffer_rows, width_dev), "expert", split_axis=0, concat_axis=0, tiled=True
    )
    down_grad = jnp.einsum(
        "jrf,jrd->jfd", hidden.reshape(rows_shape), dy_in, preferred_element_type=jnp.float32
    ).astype(jnp.bfloat16)
    expert_back = (
        jnp.einsum("jscf,jdf->sjcd", gate_delta, gate_weight, preferred_element_type=jnp.float32)
        + jnp.einsum("jscf,jdf->sjcd", up_delta, up_weight, preferred_element_type=jnp.float32)
    ).astype(jnp.bfloat16)
    grad_back = lax.all_to_all(
        expert_back.reshape(buffer_rows, width_dev), "expert", split_axis=0, concat_axis=0, tiled=True
    )
    gate_grad = jnp.einsum(
        "jrd,jrf->jdf", x_in, gate_delta.reshape(rows_shape), preferred_element_type=jnp.float32
    ).astype(jnp.bfloat16)
    up_grad = jnp.einsum(
        "jrd,jrf->jdf", x_in, up_delta.reshape(rows_shape), preferred_element_type=jnp.float32
    ).astype(jnp.bfloat16)

    flat_ids = expert_ids.reshape(slot_count)
    earlier_local = (flat_ids[None, :] == flat_ids[:, None]) & (
        position[None, :] < position[:, None]
    )
    slot_rank = jnp.sum(earlier_local.astype(jnp.int32), axis=1)
    slot_place = (flat_ids * capacity + slot_rank).reshape(token_count, per_token)
    picked_out = jnp.take(out_back, slot_place, axis=0).astype(jnp.float32)
    layer_out = jnp.sum(picked_out * route_weights[:, :, None], axis=1).astype(jnp.bfloat16)
    picked_back = jnp.take(grad_back, slot_place, axis=0).astype(jnp.float32)
    grad_tokens = jnp.sum(picked_back, axis=1).astype(jnp.bfloat16)
    return (layer_out, grad_tokens, gate_grad, up_grad, down_grad)


def solution(mesh):
    in_specs = (
        P("expert", "dp"),
        P("expert", "dp"),
        P("expert", None),
        P("expert", None),
        P("expert", "dp", None),
        P("expert", "dp", None),
        P("expert", None, "dp"),
    )
    out_specs = (
        P("expert", "dp"),
        P("expert", "dp"),
        P("expert", "dp", None),
        P("expert", "dp", None),
        P("expert", None, "dp"),
    )
    return jax.shard_map(local, mesh=mesh, in_specs=in_specs, out_specs=out_specs, check_vma=False)
```

```python
import jax
import jax.numpy as jnp
from jax import lax
from jax.sharding import PartitionSpec as P


def swiglu_parts(gate_sum, up_sum, back_sum):
    logistic = jax.nn.sigmoid(gate_sum)
    activated = gate_sum * logistic
    hidden = (activated * up_sum).astype(jnp.bfloat16)
    gate_delta = (back_sum * up_sum * logistic * (1.0 + gate_sum * (1.0 - logistic))).astype(
        jnp.bfloat16
    )
    up_delta = (back_sum * activated).astype(jnp.bfloat16)
    return (hidden, gate_delta, up_delta)


def split_f32(value):
    high = value.astype(jnp.bfloat16)
    rest = value - high.astype(jnp.float32)
    middle = rest.astype(jnp.bfloat16)
    low = (rest - middle.astype(jnp.float32)).astype(jnp.bfloat16)
    return high, middle, low


def local(tokens, out_grad, expert_ids, route_weights, gate_weight, up_weight, down_weight):
    token_count, width_dev = tokens.shape
    per_token = expert_ids.shape[1]
    local_experts = gate_weight.shape[0]
    hidden_units = gate_weight.shape[2]
    sources = lax.axis_size("expert")
    experts = local_experts * sources
    capacity = 2 * token_count * per_token // experts
    slot_count = token_count * per_token
    me = lax.axis_index("expert")

    all_tokens = sources * token_count
    least_cols = -(-1_050_000 // (2 * all_tokens))
    high, middle, low = split_f32(route_weights)
    route_cols = 4 * per_token

    def widened(parts):
        cols = sum(part.shape[1] for part in parts)
        wide = max(cols, least_cols)
        wide = wide + (-wide) % 128
        pad = jnp.zeros((token_count, wide - cols), jnp.bfloat16)
        return jnp.concatenate(parts + [pad], axis=1)

    gathered = lax.all_gather(
        widened([tokens, expert_ids.astype(jnp.bfloat16), high, middle, low]),
        "expert",
        axis=0,
        tiled=True,
    )
    tokens_all = gathered[:, :width_dev]
    route_all = gathered[:, width_dev : width_dev + route_cols].astype(jnp.float32)
    grads_all = lax.all_gather(widened([out_grad]), "expert", axis=0, tiled=True)[:, :width_dev]
    ids_all = route_all[:, :per_token].astype(jnp.int32)
    w_all = (
        route_all[:, per_token : 2 * per_token] + route_all[:, 2 * per_token : 3 * per_token]
    ) + route_all[:, 3 * per_token :]

    flat_all = ids_all.reshape(sources, slot_count)
    position = jnp.arange(slot_count, dtype=jnp.int32)
    earlier = (flat_all[:, None, :] == flat_all[:, :, None]) & (
        position[None, None, :] < position[None, :, None]
    )
    rank_all = jnp.sum(earlier.astype(jnp.int32), axis=2)
    local_e = flat_all - me * local_experts
    is_local = (local_e >= 0) & (local_e < local_experts)
    src = jnp.arange(sources, dtype=jnp.int32)[:, None]
    row_count = local_experts * sources * capacity
    row_of = jnp.where(is_local, (local_e * sources + src) * capacity + rank_all, row_count)
    row_of = row_of.reshape(sources * slot_count)
    token_of = jnp.arange(sources * slot_count, dtype=jnp.int32) // per_token
    target = jnp.arange(row_count, dtype=jnp.int32)
    hit = target[:, None] == row_of[None, :]
    holder = jnp.sum(jnp.where(hit, token_of[None, :] + 1, 0), axis=1) - 1
    row_weight = jnp.sum(jnp.where(hit, w_all.reshape(-1)[None, :], 0.0), axis=1)
    select = (holder[:, None] == jnp.arange(all_tokens, dtype=jnp.int32)[None, :]).astype(
        jnp.bfloat16
    )
    x_in = jnp.dot(select, tokens_all, preferred_element_type=jnp.float32).astype(jnp.bfloat16)
    picked_grad = jnp.dot(select, grads_all, preferred_element_type=jnp.float32)
    dy_in = (row_weight[:, None] * picked_grad).astype(jnp.bfloat16)
    x_in = x_in.reshape(local_experts, sources * capacity, width_dev)
    dy_in = dy_in.reshape(local_experts, sources * capacity, width_dev)

    gate_part = jnp.einsum(
        "jrd,jdf->jrf", x_in, gate_weight, preferred_element_type=jnp.float32
    ).astype(jnp.bfloat16)
    up_part = jnp.einsum(
        "jrd,jdf->jrf", x_in, up_weight, preferred_element_type=jnp.float32
    ).astype(jnp.bfloat16)
    front = jnp.concatenate([gate_part, up_part], axis=2).reshape(row_count, 2 * hidden_units)
    front_sums = lax.psum_scatter(front, "dp", scatter_dimension=0, tiled=True)
    back_part = jnp.einsum(
        "jrd,jfd->jrf", dy_in, down_weight, preferred_element_type=jnp.float32
    ).astype(jnp.bfloat16)
    back_sums = lax.psum_scatter(
        back_part.reshape(row_count, hidden_units), "dp", scatter_dimension=0, tiled=True
    )
    front_sums = front_sums.astype(jnp.float32)
    hidden, gate_delta, up_delta = swiglu_parts(
        front_sums[:, :hidden_units], front_sums[:, hidden_units:], back_sums.astype(jnp.float32)
    )
    hidden = lax.all_gather(hidden, "dp", axis=0, tiled=True)
    deltas = lax.all_gather(
        jnp.concatenate([gate_delta, up_delta], axis=1), "dp", axis=0, tiled=True
    )
    expert_shape = (local_experts, sources, capacity, hidden_units)
    hidden = hidden.reshape(expert_shape)
    gate_delta = deltas[:, :hidden_units].reshape(expert_shape)
    up_delta = deltas[:, hidden_units:].reshape(expert_shape)
    rows_shape = (local_experts, sources * capacity, hidden_units)

    buffer_rows = experts * capacity
    expert_out = jnp.einsum(
        "jscf,jfd->sjcd", hidden, down_weight, preferred_element_type=jnp.float32
    ).astype(jnp.bfloat16)
    out_back = lax.all_to_all(
        expert_out.reshape(buffer_rows, width_dev), "expert", split_axis=0, concat_axis=0, tiled=True
    )
    down_grad = jnp.einsum(
        "jrf,jrd->jfd", hidden.reshape(rows_shape), dy_in, preferred_element_type=jnp.float32
    ).astype(jnp.bfloat16)
    expert_back = (
        jnp.einsum("jscf,jdf->sjcd", gate_delta, gate_weight, preferred_element_type=jnp.float32)
        + jnp.einsum("jscf,jdf->sjcd", up_delta, up_weight, preferred_element_type=jnp.float32)
    ).astype(jnp.bfloat16)
    grad_back = lax.all_to_all(
        expert_back.reshape(buffer_rows, width_dev), "expert", split_axis=0, concat_axis=0, tiled=True
    )
    gate_grad = jnp.einsum(
        "jrd,jrf->jdf", x_in, gate_delta.reshape(rows_shape), preferred_element_type=jnp.float32
    ).astype(jnp.bfloat16)
    up_grad = jnp.einsum(
        "jrd,jrf->jdf", x_in, up_delta.reshape(rows_shape), preferred_element_type=jnp.float32
    ).astype(jnp.bfloat16)

    flat_ids = expert_ids.reshape(slot_count)
    earlier_local = (flat_ids[None, :] == flat_ids[:, None]) & (
        position[None, :] < position[:, None]
    )
    slot_rank = jnp.sum(earlier_local.astype(jnp.int32), axis=1)
    slot_place = (flat_ids * capacity + slot_rank).reshape(token_count, per_token)
    picked_out = jnp.take(out_back, slot_place, axis=0).astype(jnp.float32)
    layer_out = jnp.sum(picked_out * route_weights[:, :, None], axis=1).astype(jnp.bfloat16)
    picked_back = jnp.take(grad_back, slot_place, axis=0).astype(jnp.float32)
    grad_tokens = jnp.sum(picked_back, axis=1).astype(jnp.bfloat16)
    return (layer_out, grad_tokens, gate_grad, up_grad, down_grad)


def solution(mesh):
    in_specs = (
        P("expert", "dp"),
        P("expert", "dp"),
        P("expert", None),
        P("expert", None),
        P("expert", "dp", None),
        P("expert", "dp", None),
        P("expert", None, "dp"),
    )
    out_specs = (
        P("expert", "dp"),
        P("expert", "dp"),
        P("expert", "dp", None),
        P("expert", "dp", None),
        P("expert", None, "dp"),
    )
    return jax.shard_map(local, mesh=mesh, in_specs=in_specs, out_specs=out_specs, check_vma=False)
```

```python
import jax
import jax.numpy as jnp
from jax import lax
from jax.sharding import PartitionSpec as P


def swiglu_parts(gate_sum, up_sum, back_sum):
    logistic = jax.nn.sigmoid(gate_sum)
    activated = gate_sum * logistic
    hidden = (activated * up_sum).astype(jnp.bfloat16)
    gate_delta = (back_sum * up_sum * logistic * (1.0 + gate_sum * (1.0 - logistic))).astype(
        jnp.bfloat16
    )
    up_delta = (back_sum * activated).astype(jnp.bfloat16)
    return (hidden, gate_delta, up_delta)


def split_f32(value):
    high = value.astype(jnp.bfloat16)
    rest = value - high.astype(jnp.float32)
    middle = rest.astype(jnp.bfloat16)
    low = (rest - middle.astype(jnp.float32)).astype(jnp.bfloat16)
    return high, middle, low


def local(tokens, out_grad, expert_ids, route_weights, gate_weight, up_weight, down_weight):
    token_count, width_dev = tokens.shape
    per_token = expert_ids.shape[1]
    local_experts = gate_weight.shape[0]
    hidden_units = gate_weight.shape[2]
    sources = lax.axis_size("expert")
    experts = local_experts * sources
    capacity = 2 * token_count * per_token // experts
    slot_count = token_count * per_token
    me = lax.axis_index("expert")

    high, middle, low = split_f32(route_weights)
    route_cols = 4 * per_token
    pad_cols = (-route_cols) % 128
    packed = jnp.concatenate(
        [
            tokens,
            out_grad,
            expert_ids.astype(jnp.bfloat16),
            high,
            middle,
            low,
            jnp.zeros((token_count, pad_cols), jnp.bfloat16),
        ],
        axis=1,
    )
    gathered = lax.all_gather(packed, "expert", axis=0, tiled=True)
    feats = gathered[:, : 2 * width_dev]
    route_all = gathered[:, 2 * width_dev : 2 * width_dev + route_cols].astype(jnp.float32)
    ids_all = route_all[:, :per_token].astype(jnp.int32)
    w_all = (
        route_all[:, per_token : 2 * per_token] + route_all[:, 2 * per_token : 3 * per_token]
    ) + route_all[:, 3 * per_token :]
    all_tokens = sources * token_count

    flat_all = ids_all.reshape(sources, slot_count)
    position = jnp.arange(slot_count, dtype=jnp.int32)
    earlier = (flat_all[:, None, :] == flat_all[:, :, None]) & (
        position[None, None, :] < position[None, :, None]
    )
    rank_all = jnp.sum(earlier.astype(jnp.int32), axis=2)
    local_e = flat_all - me * local_experts
    is_local = (local_e >= 0) & (local_e < local_experts)
    src = jnp.arange(sources, dtype=jnp.int32)[:, None]
    row_count = local_experts * sources * capacity
    row_of = jnp.where(is_local, (local_e * sources + src) * capacity + rank_all, row_count)
    row_of = row_of.reshape(sources * slot_count)
    token_of = jnp.arange(sources * slot_count, dtype=jnp.int32) // per_token
    target = jnp.arange(row_count, dtype=jnp.int32)
    hit = target[:, None] == row_of[None, :]
    holder = jnp.sum(jnp.where(hit, token_of[None, :] + 1, 0), axis=1) - 1
    row_weight = jnp.sum(jnp.where(hit, w_all.reshape(-1)[None, :], 0.0), axis=1)
    select = (holder[:, None] == jnp.arange(all_tokens, dtype=jnp.int32)[None, :]).astype(
        jnp.bfloat16
    )
    picked = jnp.dot(select, feats, preferred_element_type=jnp.float32)
    x_in = picked[:, :width_dev].astype(jnp.bfloat16)
    dy_in = (row_weight[:, None] * picked[:, width_dev:]).astype(jnp.bfloat16)
    x_in = x_in.reshape(local_experts, sources * capacity, width_dev)
    dy_in = dy_in.reshape(local_experts, sources * capacity, width_dev)

    gate_part = jnp.einsum(
        "jrd,jdf->jrf", x_in, gate_weight, preferred_element_type=jnp.float32
    ).astype(jnp.bfloat16)
    up_part = jnp.einsum(
        "jrd,jdf->jrf", x_in, up_weight, preferred_element_type=jnp.float32
    ).astype(jnp.bfloat16)
    front = jnp.concatenate([gate_part, up_part], axis=2).reshape(row_count, 2 * hidden_units)
    front_sums = lax.psum_scatter(front, "dp", scatter_dimension=0, tiled=True)
    back_part = jnp.einsum(
        "jrd,jfd->jrf", dy_in, down_weight, preferred_element_type=jnp.float32
    ).astype(jnp.bfloat16)
    dp_count = lax.axis_size("dp")
    back_blocks = lax.all_to_all(
        back_part.reshape(row_count, hidden_units), "dp", split_axis=0, concat_axis=0, tiled=True
    )
    back_sums = jnp.sum(
        back_blocks.reshape(dp_count, row_count // dp_count, hidden_units).astype(jnp.float32),
        axis=0,
    )
    front_sums = front_sums.astype(jnp.float32)
    hidden, gate_delta, up_delta = swiglu_parts(
        front_sums[:, :hidden_units], front_sums[:, hidden_units:], back_sums
    )
    hidden = lax.all_gather(hidden, "dp", axis=0, tiled=True)
    deltas = lax.all_gather(
        jnp.concatenate([gate_delta, up_delta], axis=1), "dp", axis=0, tiled=True
    )
    expert_shape = (local_experts, sources, capacity, hidden_units)
    hidden = hidden.reshape(expert_shape)
    gate_delta = deltas[:, :hidden_units].reshape(expert_shape)
    up_delta = deltas[:, hidden_units:].reshape(expert_shape)
    rows_shape = (local_experts, sources * capacity, hidden_units)

    buffer_rows = experts * capacity
    expert_out = jnp.einsum(
        "jscf,jfd->sjcd", hidden, down_weight, preferred_element_type=jnp.float32
    ).astype(jnp.bfloat16)
    out_back = lax.all_to_all(
        expert_out.reshape(buffer_rows, width_dev), "expert", split_axis=0, concat_axis=0, tiled=True
    )
    down_grad = jnp.einsum(
        "jrf,jrd->jfd", hidden.reshape(rows_shape), dy_in, preferred_element_type=jnp.float32
    ).astype(jnp.bfloat16)
    expert_back = (
        jnp.einsum("jscf,jdf->sjcd", gate_delta, gate_weight, preferred_element_type=jnp.float32)
        + jnp.einsum("jscf,jdf->sjcd", up_delta, up_weight, preferred_element_type=jnp.float32)
    ).astype(jnp.bfloat16)
    grad_back = lax.all_to_all(
        expert_back.reshape(buffer_rows, width_dev), "expert", split_axis=0, concat_axis=0, tiled=True
    )
    gate_grad = jnp.einsum(
        "jrd,jrf->jdf", x_in, gate_delta.reshape(rows_shape), preferred_element_type=jnp.float32
    ).astype(jnp.bfloat16)
    up_grad = jnp.einsum(
        "jrd,jrf->jdf", x_in, up_delta.reshape(rows_shape), preferred_element_type=jnp.float32
    ).astype(jnp.bfloat16)

    flat_ids = expert_ids.reshape(slot_count)
    earlier_local = (flat_ids[None, :] == flat_ids[:, None]) & (
        position[None, :] < position[:, None]
    )
    slot_rank = jnp.sum(earlier_local.astype(jnp.int32), axis=1)
    slot_place = (flat_ids * capacity + slot_rank).reshape(token_count, per_token)
    picked_out = jnp.take(out_back, slot_place, axis=0).astype(jnp.float32)
    layer_out = jnp.sum(picked_out * route_weights[:, :, None], axis=1).astype(jnp.bfloat16)
    picked_back = jnp.take(grad_back, slot_place, axis=0).astype(jnp.float32)
    grad_tokens = jnp.sum(picked_back, axis=1).astype(jnp.bfloat16)
    return (layer_out, grad_tokens, gate_grad, up_grad, down_grad)


def solution(mesh):
    in_specs = (
        P("expert", "dp"),
        P("expert", "dp"),
        P("expert", None),
        P("expert", None),
        P("expert", "dp", None),
        P("expert", "dp", None),
        P("expert", None, "dp"),
    )
    out_specs = (
        P("expert", "dp"),
        P("expert", "dp"),
        P("expert", "dp", None),
        P("expert", "dp", None),
        P("expert", None, "dp"),
    )
    return jax.shard_map(local, mesh=mesh, in_specs=in_specs, out_specs=out_specs, check_vma=False)
```

```python
import jax
import jax.numpy as jnp
from jax import lax
from jax.sharding import PartitionSpec as P


def swiglu_parts(gate_sum, up_sum, back_sum):
    logistic = jax.nn.sigmoid(gate_sum)
    activated = gate_sum * logistic
    hidden = (activated * up_sum).astype(jnp.bfloat16)
    gate_delta = (back_sum * up_sum * logistic * (1.0 + gate_sum * (1.0 - logistic))).astype(
        jnp.bfloat16
    )
    up_delta = (back_sum * activated).astype(jnp.bfloat16)
    return (hidden, gate_delta, up_delta)


def split_f32(value):
    high = value.astype(jnp.bfloat16)
    rest = value - high.astype(jnp.float32)
    middle = rest.astype(jnp.bfloat16)
    low = (rest - middle.astype(jnp.float32)).astype(jnp.bfloat16)
    return high, middle, low


def local(tokens, out_grad, expert_ids, route_weights, gate_weight, up_weight, down_weight):
    token_count, width_dev = tokens.shape
    per_token = expert_ids.shape[1]
    local_experts = gate_weight.shape[0]
    hidden_units = gate_weight.shape[2]
    sources = lax.axis_size("expert")
    experts = local_experts * sources
    capacity = 2 * token_count * per_token // experts
    slot_count = token_count * per_token
    me = lax.axis_index("expert")

    high, middle, low = split_f32(route_weights)
    route_cols = 4 * per_token
    pad_cols = (-route_cols) % 128
    packed = jnp.concatenate(
        [
            tokens,
            out_grad,
            expert_ids.astype(jnp.bfloat16),
            high,
            middle,
            low,
            jnp.zeros((token_count, pad_cols), jnp.bfloat16),
        ],
        axis=1,
    )
    gathered = lax.all_gather(packed, "expert", axis=0, tiled=True)
    feats = gathered[:, : 2 * width_dev]
    route_all = gathered[:, 2 * width_dev : 2 * width_dev + route_cols].astype(jnp.float32)
    ids_all = route_all[:, :per_token].astype(jnp.int32)
    w_all = (
        route_all[:, per_token : 2 * per_token] + route_all[:, 2 * per_token : 3 * per_token]
    ) + route_all[:, 3 * per_token :]
    all_tokens = sources * token_count

    flat_all = ids_all.reshape(sources, slot_count)
    position = jnp.arange(slot_count, dtype=jnp.int32)
    earlier = (flat_all[:, None, :] == flat_all[:, :, None]) & (
        position[None, None, :] < position[None, :, None]
    )
    rank_all = jnp.sum(earlier.astype(jnp.int32), axis=2)
    local_e = flat_all - me * local_experts
    is_local = (local_e >= 0) & (local_e < local_experts)
    src = jnp.arange(sources, dtype=jnp.int32)[:, None]
    row_count = local_experts * sources * capacity
    row_of = jnp.where(is_local, (local_e * sources + src) * capacity + rank_all, row_count)
    row_of = row_of.reshape(sources * slot_count)
    token_of = jnp.arange(sources * slot_count, dtype=jnp.int32) // per_token
    target = jnp.arange(row_count, dtype=jnp.int32)
    hit = target[:, None] == row_of[None, :]
    holder = jnp.sum(jnp.where(hit, token_of[None, :] + 1, 0), axis=1) - 1
    row_weight = jnp.sum(jnp.where(hit, w_all.reshape(-1)[None, :], 0.0), axis=1)
    select = (holder[:, None] == jnp.arange(all_tokens, dtype=jnp.int32)[None, :]).astype(
        jnp.bfloat16
    )
    picked = jnp.dot(select, feats, preferred_element_type=jnp.float32)
    x_in = picked[:, :width_dev].astype(jnp.bfloat16)
    dy_in = (row_weight[:, None] * picked[:, width_dev:]).astype(jnp.bfloat16)
    x_in = x_in.reshape(local_experts, sources * capacity, width_dev)
    dy_in = dy_in.reshape(local_experts, sources * capacity, width_dev)

    gate_part = jnp.einsum(
        "jrd,jdf->jrf", x_in, gate_weight, preferred_element_type=jnp.float32
    ).astype(jnp.bfloat16)
    up_part = jnp.einsum(
        "jrd,jdf->jrf", x_in, up_weight, preferred_element_type=jnp.float32
    ).astype(jnp.bfloat16)
    front = jnp.concatenate([gate_part, up_part], axis=2).reshape(row_count, 2 * hidden_units)
    front_sums = lax.psum_scatter(front, "dp", scatter_dimension=0, tiled=True)
    back_part = jnp.einsum(
        "jrd,jfd->jrf", dy_in, down_weight, preferred_element_type=jnp.float32
    ).astype(jnp.bfloat16)
    dp_count = lax.axis_size("dp")
    back_blocks = lax.all_to_all(
        back_part.reshape(row_count, hidden_units), "dp", split_axis=0, concat_axis=0, tiled=True
    )
    back_sums = jnp.sum(
        back_blocks.reshape(dp_count, row_count // dp_count, hidden_units).astype(jnp.float32),
        axis=0,
    )
    front_sums = front_sums.astype(jnp.float32)
    hidden, gate_delta, up_delta = swiglu_parts(
        front_sums[:, :hidden_units], front_sums[:, hidden_units:], back_sums
    )
    first = lax.all_gather(
        jnp.concatenate([hidden, gate_delta], axis=1), "dp", axis=0, tiled=True
    )
    up_delta, first = lax.optimization_barrier((up_delta, first))
    up_delta = lax.all_gather(up_delta, "dp", axis=0, tiled=True)
    rows_shape = (local_experts, sources * capacity, hidden_units)
    expert_shape = (local_experts, sources, capacity, hidden_units)
    hidden = first[:, :hidden_units]
    gate_delta = first[:, hidden_units:]

    buffer_rows = experts * capacity
    expert_out = jnp.einsum(
        "jscf,jfd->sjcd", hidden.reshape(expert_shape), down_weight,
        preferred_element_type=jnp.float32,
    ).astype(jnp.bfloat16)
    out_back = lax.all_to_all(
        expert_out.reshape(buffer_rows, width_dev), "expert", split_axis=0, concat_axis=0, tiled=True
    )
    down_grad = jnp.einsum(
        "jrf,jrd->jfd", hidden.reshape(rows_shape), dy_in, preferred_element_type=jnp.float32
    ).astype(jnp.bfloat16)
    gate_back = lax.optimization_barrier(
        jnp.einsum(
            "jscf,jdf->sjcd", gate_delta.reshape(expert_shape), gate_weight,
            preferred_element_type=jnp.float32,
        )
    )
    gate_grad = jnp.einsum(
        "jrd,jrf->jdf", x_in, gate_delta.reshape(rows_shape), preferred_element_type=jnp.float32
    ).astype(jnp.bfloat16)
    expert_back = (
        gate_back
        + jnp.einsum(
            "jscf,jdf->sjcd", up_delta.reshape(expert_shape), up_weight,
            preferred_element_type=jnp.float32,
        )
    ).astype(jnp.bfloat16)
    grad_back = lax.all_to_all(
        expert_back.reshape(buffer_rows, width_dev), "expert", split_axis=0, concat_axis=0, tiled=True
    )
    up_grad = jnp.einsum(
        "jrd,jrf->jdf", x_in, up_delta.reshape(rows_shape), preferred_element_type=jnp.float32
    ).astype(jnp.bfloat16)

    flat_ids = expert_ids.reshape(slot_count)
    earlier_local = (flat_ids[None, :] == flat_ids[:, None]) & (
        position[None, :] < position[:, None]
    )
    slot_rank = jnp.sum(earlier_local.astype(jnp.int32), axis=1)
    slot_place = (flat_ids * capacity + slot_rank).reshape(token_count, per_token)
    picked_out = jnp.take(out_back, slot_place, axis=0).astype(jnp.float32)
    layer_out = jnp.sum(picked_out * route_weights[:, :, None], axis=1).astype(jnp.bfloat16)
    picked_back = jnp.take(grad_back, slot_place, axis=0).astype(jnp.float32)
    grad_tokens = jnp.sum(picked_back, axis=1).astype(jnp.bfloat16)
    return (layer_out, grad_tokens, gate_grad, up_grad, down_grad)


def solution(mesh):
    in_specs = (
        P("expert", "dp"),
        P("expert", "dp"),
        P("expert", None),
        P("expert", None),
        P("expert", "dp", None),
        P("expert", "dp", None),
        P("expert", None, "dp"),
    )
    out_specs = (
        P("expert", "dp"),
        P("expert", "dp"),
        P("expert", "dp", None),
        P("expert", "dp", None),
        P("expert", None, "dp"),
    )
    return jax.shard_map(local, mesh=mesh, in_specs=in_specs, out_specs=out_specs, check_vma=False)
```

```python
import jax
import jax.numpy as jnp
from jax import lax
from jax.sharding import PartitionSpec as P


def swiglu_parts(gate_sum, up_sum, back_sum):
    logistic = jax.nn.sigmoid(gate_sum)
    activated = gate_sum * logistic
    hidden = (activated * up_sum).astype(jnp.bfloat16)
    gate_delta = (back_sum * up_sum * logistic * (1.0 + gate_sum * (1.0 - logistic))).astype(
        jnp.bfloat16
    )
    up_delta = (back_sum * activated).astype(jnp.bfloat16)
    return (hidden, gate_delta, up_delta)


def split_f32(value):
    high = value.astype(jnp.bfloat16)
    rest = value - high.astype(jnp.float32)
    middle = rest.astype(jnp.bfloat16)
    low = (rest - middle.astype(jnp.float32)).astype(jnp.bfloat16)
    return high, middle, low


def local(tokens, out_grad, expert_ids, route_weights, gate_weight, up_weight, down_weight):
    token_count, width_dev = tokens.shape
    per_token = expert_ids.shape[1]
    local_experts = gate_weight.shape[0]
    hidden_units = gate_weight.shape[2]
    sources = lax.axis_size("expert")
    experts = local_experts * sources
    capacity = 2 * token_count * per_token // experts
    slot_count = token_count * per_token
    me = lax.axis_index("expert")

    high, middle, low = split_f32(route_weights)
    route_cols = 4 * per_token
    pad_cols = (-route_cols) % 128
    packed = jnp.concatenate(
        [
            tokens,
            out_grad,
            expert_ids.astype(jnp.bfloat16),
            high,
            middle,
            low,
            jnp.zeros((token_count, pad_cols), jnp.bfloat16),
        ],
        axis=1,
    )
    gathered = lax.all_gather(packed, "expert", axis=0, tiled=True)
    feats = gathered[:, : 2 * width_dev]
    route_all = gathered[:, 2 * width_dev : 2 * width_dev + route_cols].astype(jnp.float32)
    ids_all = route_all[:, :per_token].astype(jnp.int32)
    w_all = (
        route_all[:, per_token : 2 * per_token] + route_all[:, 2 * per_token : 3 * per_token]
    ) + route_all[:, 3 * per_token :]
    all_tokens = sources * token_count

    flat_all = ids_all.reshape(sources, slot_count)
    position = jnp.arange(slot_count, dtype=jnp.int32)
    earlier = (flat_all[:, None, :] == flat_all[:, :, None]) & (
        position[None, None, :] < position[None, :, None]
    )
    rank_all = jnp.sum(earlier.astype(jnp.int32), axis=2)
    local_e = flat_all - me * local_experts
    is_local = (local_e >= 0) & (local_e < local_experts)
    src = jnp.arange(sources, dtype=jnp.int32)[:, None]
    row_count = local_experts * sources * capacity
    row_of = jnp.where(is_local, (local_e * sources + src) * capacity + rank_all, row_count)
    row_of = row_of.reshape(sources * slot_count)
    token_of = jnp.arange(sources * slot_count, dtype=jnp.int32) // per_token
    target = jnp.arange(row_count, dtype=jnp.int32)
    hit = target[:, None] == row_of[None, :]
    holder = jnp.sum(jnp.where(hit, token_of[None, :] + 1, 0), axis=1) - 1
    row_weight = jnp.sum(jnp.where(hit, w_all.reshape(-1)[None, :], 0.0), axis=1)
    select = (holder[:, None] == jnp.arange(all_tokens, dtype=jnp.int32)[None, :]).astype(
        jnp.bfloat16
    )
    picked = jnp.dot(select, feats, preferred_element_type=jnp.float32)
    x_in = picked[:, :width_dev].astype(jnp.bfloat16)
    dy_in = (row_weight[:, None] * picked[:, width_dev:]).astype(jnp.bfloat16)
    x_in = x_in.reshape(local_experts, sources * capacity, width_dev)
    dy_in = dy_in.reshape(local_experts, sources * capacity, width_dev)

    gate_part = jnp.einsum(
        "jrd,jdf->jrf", x_in, gate_weight, preferred_element_type=jnp.float32
    ).astype(jnp.bfloat16)
    up_part = jnp.einsum(
        "jrd,jdf->jrf", x_in, up_weight, preferred_element_type=jnp.float32
    ).astype(jnp.bfloat16)
    front = jnp.concatenate([gate_part, up_part], axis=2).reshape(row_count, 2 * hidden_units)
    front_sums = lax.psum_scatter(front, "dp", scatter_dimension=0, tiled=True)
    back_part = jnp.einsum(
        "jrd,jfd->jrf", dy_in, down_weight, preferred_element_type=jnp.float32
    ).astype(jnp.bfloat16)
    dp_count = lax.axis_size("dp")
    back_blocks = lax.all_to_all(
        back_part.reshape(row_count, hidden_units), "dp", split_axis=0, concat_axis=0, tiled=True
    )
    back_sums = jnp.sum(
        back_blocks.reshape(dp_count, row_count // dp_count, hidden_units).astype(jnp.float32),
        axis=0,
    )
    front_sums = front_sums.astype(jnp.float32)
    hidden, gate_delta, up_delta = swiglu_parts(
        front_sums[:, :hidden_units], front_sums[:, hidden_units:], back_sums
    )
    deltas = lax.all_gather(
        jnp.concatenate([gate_delta, up_delta], axis=1), "dp", axis=0, tiled=True
    )
    hidden = lax.all_to_all(
        jnp.broadcast_to(hidden[None], (dp_count,) + hidden.shape).reshape(
            dp_count * hidden.shape[0], hidden_units
        ),
        "dp",
        split_axis=0,
        concat_axis=0,
        tiled=True,
    )
    expert_shape = (local_experts, sources, capacity, hidden_units)
    hidden = hidden.reshape(expert_shape)
    gate_delta = deltas[:, :hidden_units].reshape(expert_shape)
    up_delta = deltas[:, hidden_units:].reshape(expert_shape)
    rows_shape = (local_experts, sources * capacity, hidden_units)

    buffer_rows = experts * capacity
    expert_out = jnp.einsum(
        "jscf,jfd->sjcd", hidden, down_weight, preferred_element_type=jnp.float32
    ).astype(jnp.bfloat16)
    out_back = lax.all_to_all(
        expert_out.reshape(buffer_rows, width_dev), "expert", split_axis=0, concat_axis=0, tiled=True
    )
    down_grad = jnp.einsum(
        "jrf,jrd->jfd", hidden.reshape(rows_shape), dy_in, preferred_element_type=jnp.float32
    ).astype(jnp.bfloat16)
    expert_back = (
        jnp.einsum("jscf,jdf->sjcd", gate_delta, gate_weight, preferred_element_type=jnp.float32)
        + jnp.einsum("jscf,jdf->sjcd", up_delta, up_weight, preferred_element_type=jnp.float32)
    ).astype(jnp.bfloat16)
    grad_back = lax.all_to_all(
        expert_back.reshape(buffer_rows, width_dev), "expert", split_axis=0, concat_axis=0, tiled=True
    )
    gate_grad = jnp.einsum(
        "jrd,jrf->jdf", x_in, gate_delta.reshape(rows_shape), preferred_element_type=jnp.float32
    ).astype(jnp.bfloat16)
    up_grad = jnp.einsum(
        "jrd,jrf->jdf", x_in, up_delta.reshape(rows_shape), preferred_element_type=jnp.float32
    ).astype(jnp.bfloat16)

    flat_ids = expert_ids.reshape(slot_count)
    earlier_local = (flat_ids[None, :] == flat_ids[:, None]) & (
        position[None, :] < position[:, None]
    )
    slot_rank = jnp.sum(earlier_local.astype(jnp.int32), axis=1)
    slot_place = (flat_ids * capacity + slot_rank).reshape(token_count, per_token)
    picked_out = jnp.take(out_back, slot_place, axis=0).astype(jnp.float32)
    layer_out = jnp.sum(picked_out * route_weights[:, :, None], axis=1).astype(jnp.bfloat16)
    picked_back = jnp.take(grad_back, slot_place, axis=0).astype(jnp.float32)
    grad_tokens = jnp.sum(picked_back, axis=1).astype(jnp.bfloat16)
    return (layer_out, grad_tokens, gate_grad, up_grad, down_grad)


def solution(mesh):
    in_specs = (
        P("expert", "dp"),
        P("expert", "dp"),
        P("expert", None),
        P("expert", None),
        P("expert", "dp", None),
        P("expert", "dp", None),
        P("expert", None, "dp"),
    )
    out_specs = (
        P("expert", "dp"),
        P("expert", "dp"),
        P("expert", "dp", None),
        P("expert", "dp", None),
        P("expert", None, "dp"),
    )
    return jax.shard_map(local, mesh=mesh, in_specs=in_specs, out_specs=out_specs, check_vma=False)
```

```python
import jax
import jax.numpy as jnp
from jax import lax
from jax.sharding import PartitionSpec as P


def swiglu_parts(gate_sum, up_sum, back_sum):
    logistic = jax.nn.sigmoid(gate_sum)
    activated = gate_sum * logistic
    hidden = (activated * up_sum).astype(jnp.bfloat16)
    gate_delta = (back_sum * up_sum * logistic * (1.0 + gate_sum * (1.0 - logistic))).astype(
        jnp.bfloat16
    )
    up_delta = (back_sum * activated).astype(jnp.bfloat16)
    return (hidden, gate_delta, up_delta)


def split_f32(value):
    high = value.astype(jnp.bfloat16)
    rest = value - high.astype(jnp.float32)
    middle = rest.astype(jnp.bfloat16)
    low = (rest - middle.astype(jnp.float32)).astype(jnp.bfloat16)
    return high, middle, low


def local(tokens, out_grad, expert_ids, route_weights, gate_weight, up_weight, down_weight):
    token_count, width_dev = tokens.shape
    per_token = expert_ids.shape[1]
    local_experts = gate_weight.shape[0]
    hidden_units = gate_weight.shape[2]
    sources = lax.axis_size("expert")
    experts = local_experts * sources
    capacity = 2 * token_count * per_token // experts
    slot_count = token_count * per_token
    me = lax.axis_index("expert")

    high, middle, low = split_f32(route_weights)
    route_cols = 4 * per_token
    pad_cols = (-route_cols) % 128
    packed = jnp.concatenate(
        [
            tokens,
            out_grad,
            expert_ids.astype(jnp.bfloat16),
            high,
            middle,
            low,
            jnp.zeros((token_count, pad_cols), jnp.bfloat16),
        ],
        axis=1,
    )
    gathered = lax.all_to_all(
        jnp.broadcast_to(packed[None], (sources,) + packed.shape).reshape(
            sources * token_count, packed.shape[1]
        ),
        "expert",
        split_axis=0,
        concat_axis=0,
        tiled=True,
    )
    feats = gathered[:, : 2 * width_dev]
    route_all = gathered[:, 2 * width_dev : 2 * width_dev + route_cols].astype(jnp.float32)
    ids_all = route_all[:, :per_token].astype(jnp.int32)
    w_all = (
        route_all[:, per_token : 2 * per_token] + route_all[:, 2 * per_token : 3 * per_token]
    ) + route_all[:, 3 * per_token :]
    all_tokens = sources * token_count

    flat_all = ids_all.reshape(sources, slot_count)
    position = jnp.arange(slot_count, dtype=jnp.int32)
    earlier = (flat_all[:, None, :] == flat_all[:, :, None]) & (
        position[None, None, :] < position[None, :, None]
    )
    rank_all = jnp.sum(earlier.astype(jnp.int32), axis=2)
    local_e = flat_all - me * local_experts
    is_local = (local_e >= 0) & (local_e < local_experts)
    src = jnp.arange(sources, dtype=jnp.int32)[:, None]
    row_count = local_experts * sources * capacity
    row_of = jnp.where(is_local, (local_e * sources + src) * capacity + rank_all, row_count)
    row_of = row_of.reshape(sources * slot_count)
    token_of = jnp.arange(sources * slot_count, dtype=jnp.int32) // per_token
    target = jnp.arange(row_count, dtype=jnp.int32)
    hit = target[:, None] == row_of[None, :]
    holder = jnp.sum(jnp.where(hit, token_of[None, :] + 1, 0), axis=1) - 1
    row_weight = jnp.sum(jnp.where(hit, w_all.reshape(-1)[None, :], 0.0), axis=1)
    select = (holder[:, None] == jnp.arange(all_tokens, dtype=jnp.int32)[None, :]).astype(
        jnp.bfloat16
    )
    picked = jnp.dot(select, feats, preferred_element_type=jnp.float32)
    x_in = picked[:, :width_dev].astype(jnp.bfloat16)
    dy_in = (row_weight[:, None] * picked[:, width_dev:]).astype(jnp.bfloat16)
    x_in = x_in.reshape(local_experts, sources * capacity, width_dev)
    dy_in = dy_in.reshape(local_experts, sources * capacity, width_dev)

    gate_part = jnp.einsum(
        "jrd,jdf->jrf", x_in, gate_weight, preferred_element_type=jnp.float32
    ).astype(jnp.bfloat16)
    up_part = jnp.einsum(
        "jrd,jdf->jrf", x_in, up_weight, preferred_element_type=jnp.float32
    ).astype(jnp.bfloat16)
    front = jnp.concatenate([gate_part, up_part], axis=2).reshape(row_count, 2 * hidden_units)
    front_sums = lax.psum_scatter(front, "dp", scatter_dimension=0, tiled=True)
    back_part = jnp.einsum(
        "jrd,jfd->jrf", dy_in, down_weight, preferred_element_type=jnp.float32
    ).astype(jnp.bfloat16)
    dp_count = lax.axis_size("dp")
    back_blocks = lax.all_to_all(
        back_part.reshape(row_count, hidden_units), "dp", split_axis=0, concat_axis=0, tiled=True
    )
    back_sums = jnp.sum(
        back_blocks.reshape(dp_count, row_count // dp_count, hidden_units).astype(jnp.float32),
        axis=0,
    )
    front_sums = front_sums.astype(jnp.float32)
    hidden, gate_delta, up_delta = swiglu_parts(
        front_sums[:, :hidden_units], front_sums[:, hidden_units:], back_sums
    )
    hidden = lax.all_gather(hidden, "dp", axis=0, tiled=True)
    deltas = lax.all_gather(
        jnp.concatenate([gate_delta, up_delta], axis=1), "dp", axis=0, tiled=True
    )
    expert_shape = (local_experts, sources, capacity, hidden_units)
    hidden = hidden.reshape(expert_shape)
    gate_delta = deltas[:, :hidden_units].reshape(expert_shape)
    up_delta = deltas[:, hidden_units:].reshape(expert_shape)
    rows_shape = (local_experts, sources * capacity, hidden_units)

    buffer_rows = experts * capacity
    expert_out = jnp.einsum(
        "jscf,jfd->sjcd", hidden, down_weight, preferred_element_type=jnp.float32
    ).astype(jnp.bfloat16)
    out_back = lax.all_to_all(
        expert_out.reshape(buffer_rows, width_dev), "expert", split_axis=0, concat_axis=0, tiled=True
    )
    down_grad = jnp.einsum(
        "jrf,jrd->jfd", hidden.reshape(rows_shape), dy_in, preferred_element_type=jnp.float32
    ).astype(jnp.bfloat16)
    expert_back = (
        jnp.einsum("jscf,jdf->sjcd", gate_delta, gate_weight, preferred_element_type=jnp.float32)
        + jnp.einsum("jscf,jdf->sjcd", up_delta, up_weight, preferred_element_type=jnp.float32)
    ).astype(jnp.bfloat16)
    grad_back = lax.all_to_all(
        expert_back.reshape(buffer_rows, width_dev), "expert", split_axis=0, concat_axis=0, tiled=True
    )
    gate_grad = jnp.einsum(
        "jrd,jrf->jdf", x_in, gate_delta.reshape(rows_shape), preferred_element_type=jnp.float32
    ).astype(jnp.bfloat16)
    up_grad = jnp.einsum(
        "jrd,jrf->jdf", x_in, up_delta.reshape(rows_shape), preferred_element_type=jnp.float32
    ).astype(jnp.bfloat16)

    flat_ids = expert_ids.reshape(slot_count)
    earlier_local = (flat_ids[None, :] == flat_ids[:, None]) & (
        position[None, :] < position[:, None]
    )
    slot_rank = jnp.sum(earlier_local.astype(jnp.int32), axis=1)
    slot_place = (flat_ids * capacity + slot_rank).reshape(token_count, per_token)
    picked_out = jnp.take(out_back, slot_place, axis=0).astype(jnp.float32)
    layer_out = jnp.sum(picked_out * route_weights[:, :, None], axis=1).astype(jnp.bfloat16)
    picked_back = jnp.take(grad_back, slot_place, axis=0).astype(jnp.float32)
    grad_tokens = jnp.sum(picked_back, axis=1).astype(jnp.bfloat16)
    return (layer_out, grad_tokens, gate_grad, up_grad, down_grad)


def solution(mesh):
    in_specs = (
        P("expert", "dp"),
        P("expert", "dp"),
        P("expert", None),
        P("expert", None),
        P("expert", "dp", None),
        P("expert", "dp", None),
        P("expert", None, "dp"),
    )
    out_specs = (
        P("expert", "dp"),
        P("expert", "dp"),
        P("expert", "dp", None),
        P("expert", "dp", None),
        P("expert", None, "dp"),
    )
    return jax.shard_map(local, mesh=mesh, in_specs=in_specs, out_specs=out_specs, check_vma=False)
```

```python
import jax
import jax.numpy as jnp
from jax import lax
from jax.sharding import PartitionSpec as P


def swiglu_parts(gate_sum, up_sum, back_sum):
    logistic = jax.nn.sigmoid(gate_sum)
    activated = gate_sum * logistic
    hidden = (activated * up_sum).astype(jnp.bfloat16)
    gate_delta = (back_sum * up_sum * logistic * (1.0 + gate_sum * (1.0 - logistic))).astype(
        jnp.bfloat16
    )
    up_delta = (back_sum * activated).astype(jnp.bfloat16)
    return (hidden, gate_delta, up_delta)


def split_f32(value):
    high = value.astype(jnp.bfloat16)
    rest = value - high.astype(jnp.float32)
    middle = rest.astype(jnp.bfloat16)
    low = (rest - middle.astype(jnp.float32)).astype(jnp.bfloat16)
    return high, middle, low


def local(tokens, out_grad, expert_ids, route_weights, gate_weight, up_weight, down_weight):
    token_count, width_dev = tokens.shape
    per_token = expert_ids.shape[1]
    local_experts = gate_weight.shape[0]
    hidden_units = gate_weight.shape[2]
    sources = lax.axis_size("expert")
    experts = local_experts * sources
    capacity = 2 * token_count * per_token // experts
    slot_count = token_count * per_token
    me = lax.axis_index("expert")

    high, middle, low = split_f32(route_weights)
    route_cols = 4 * per_token
    pad_cols = (-route_cols) % 128
    packed = jnp.concatenate(
        [
            tokens,
            out_grad,
            expert_ids.astype(jnp.bfloat16),
            high,
            middle,
            low,
            jnp.zeros((token_count, pad_cols), jnp.bfloat16),
        ],
        axis=1,
    )
    gathered = lax.all_to_all(
        jnp.broadcast_to(packed[None], (sources,) + packed.shape).reshape(
            sources * token_count, packed.shape[1]
        ),
        "expert",
        split_axis=0,
        concat_axis=0,
        tiled=True,
    )
    feats = gathered[:, : 2 * width_dev]
    route_all = gathered[:, 2 * width_dev : 2 * width_dev + route_cols].astype(jnp.float32)
    ids_all = route_all[:, :per_token].astype(jnp.int32)
    w_all = (
        route_all[:, per_token : 2 * per_token] + route_all[:, 2 * per_token : 3 * per_token]
    ) + route_all[:, 3 * per_token :]
    all_tokens = sources * token_count

    flat_all = ids_all.reshape(sources, slot_count)
    position = jnp.arange(slot_count, dtype=jnp.int32)
    earlier = (flat_all[:, None, :] == flat_all[:, :, None]) & (
        position[None, None, :] < position[None, :, None]
    )
    rank_all = jnp.sum(earlier.astype(jnp.int32), axis=2)
    local_e = flat_all - me * local_experts
    is_local = (local_e >= 0) & (local_e < local_experts)
    src = jnp.arange(sources, dtype=jnp.int32)[:, None]
    row_count = local_experts * sources * capacity
    row_of = jnp.where(is_local, (local_e * sources + src) * capacity + rank_all, row_count)
    row_of = row_of.reshape(sources * slot_count)
    token_of = jnp.arange(sources * slot_count, dtype=jnp.int32) // per_token
    target = jnp.arange(row_count, dtype=jnp.int32)
    hit = target[:, None] == row_of[None, :]
    holder = jnp.sum(jnp.where(hit, token_of[None, :] + 1, 0), axis=1) - 1
    row_weight = jnp.sum(jnp.where(hit, w_all.reshape(-1)[None, :], 0.0), axis=1)
    select = (holder[:, None] == jnp.arange(all_tokens, dtype=jnp.int32)[None, :]).astype(
        jnp.bfloat16
    )
    picked = jnp.dot(select, feats, preferred_element_type=jnp.float32)
    x_in = picked[:, :width_dev].astype(jnp.bfloat16)
    dy_in = (row_weight[:, None] * picked[:, width_dev:]).astype(jnp.bfloat16)
    x_in = x_in.reshape(local_experts, sources * capacity, width_dev)
    dy_in = dy_in.reshape(local_experts, sources * capacity, width_dev)

    gate_part = jnp.einsum(
        "jrd,jdf->jrf", x_in, gate_weight, preferred_element_type=jnp.float32
    ).astype(jnp.bfloat16)
    up_part = jnp.einsum(
        "jrd,jdf->jrf", x_in, up_weight, preferred_element_type=jnp.float32
    ).astype(jnp.bfloat16)
    front = jnp.concatenate([gate_part, up_part], axis=2).reshape(row_count, 2 * hidden_units)
    front_sums = lax.psum_scatter(front, "dp", scatter_dimension=0, tiled=True)
    back_part = jnp.einsum(
        "jrd,jfd->jrf", dy_in, down_weight, preferred_element_type=jnp.float32
    ).astype(jnp.bfloat16)
    dp_count = lax.axis_size("dp")
    back_blocks = lax.all_to_all(
        back_part.reshape(row_count, hidden_units), "dp", split_axis=0, concat_axis=0, tiled=True
    )
    back_sums = jnp.sum(
        back_blocks.reshape(dp_count, row_count // dp_count, hidden_units).astype(jnp.float32),
        axis=0,
    )
    front_sums = front_sums.astype(jnp.float32)
    hidden, gate_delta, up_delta = swiglu_parts(
        front_sums[:, :hidden_units], front_sums[:, hidden_units:], back_sums
    )
    hidden = lax.all_gather(hidden, "dp", axis=0, tiled=True)
    deltas = lax.all_gather(
        jnp.concatenate([gate_delta, up_delta], axis=1), "dp", axis=0, tiled=True
    )
    expert_shape = (local_experts, sources, capacity, hidden_units)
    hidden = hidden.reshape(expert_shape)
    gate_delta = deltas[:, :hidden_units].reshape(expert_shape)
    up_delta = deltas[:, hidden_units:].reshape(expert_shape)
    rows_shape = (local_experts, sources * capacity, hidden_units)

    buffer_rows = experts * capacity
    expert_out = jnp.einsum(
        "jrf,jfd->jrd", hidden.reshape(rows_shape), down_weight, preferred_element_type=jnp.float32
    ).astype(jnp.bfloat16)
    expert_out = expert_out.reshape(local_experts, sources, capacity, width_dev).transpose(1, 0, 2, 3)
    out_back = lax.all_to_all(
        expert_out.reshape(buffer_rows, width_dev), "expert", split_axis=0, concat_axis=0, tiled=True
    )
    down_grad = jnp.einsum(
        "jrf,jrd->jfd", hidden.reshape(rows_shape), dy_in, preferred_element_type=jnp.float32
    ).astype(jnp.bfloat16)
    expert_back = (
        jnp.einsum(
            "jrf,jdf->jrd", gate_delta.reshape(rows_shape), gate_weight,
            preferred_element_type=jnp.float32,
        )
        + jnp.einsum(
            "jrf,jdf->jrd", up_delta.reshape(rows_shape), up_weight,
            preferred_element_type=jnp.float32,
        )
    ).astype(jnp.bfloat16)
    expert_back = expert_back.reshape(local_experts, sources, capacity, width_dev).transpose(
        1, 0, 2, 3
    )
    grad_back = lax.all_to_all(
        expert_back.reshape(buffer_rows, width_dev), "expert", split_axis=0, concat_axis=0, tiled=True
    )
    gate_grad = jnp.einsum(
        "jrd,jrf->jdf", x_in, gate_delta.reshape(rows_shape), preferred_element_type=jnp.float32
    ).astype(jnp.bfloat16)
    up_grad = jnp.einsum(
        "jrd,jrf->jdf", x_in, up_delta.reshape(rows_shape), preferred_element_type=jnp.float32
    ).astype(jnp.bfloat16)

    flat_ids = expert_ids.reshape(slot_count)
    earlier_local = (flat_ids[None, :] == flat_ids[:, None]) & (
        position[None, :] < position[:, None]
    )
    slot_rank = jnp.sum(earlier_local.astype(jnp.int32), axis=1)
    slot_place = (flat_ids * capacity + slot_rank).reshape(token_count, per_token)
    picked_out = jnp.take(out_back, slot_place, axis=0).astype(jnp.float32)
    layer_out = jnp.sum(picked_out * route_weights[:, :, None], axis=1).astype(jnp.bfloat16)
    picked_back = jnp.take(grad_back, slot_place, axis=0).astype(jnp.float32)
    grad_tokens = jnp.sum(picked_back, axis=1).astype(jnp.bfloat16)
    return (layer_out, grad_tokens, gate_grad, up_grad, down_grad)


def solution(mesh):
    in_specs = (
        P("expert", "dp"),
        P("expert", "dp"),
        P("expert", None),
        P("expert", None),
        P("expert", "dp", None),
        P("expert", "dp", None),
        P("expert", None, "dp"),
    )
    out_specs = (
        P("expert", "dp"),
        P("expert", "dp"),
        P("expert", "dp", None),
        P("expert", "dp", None),
        P("expert", None, "dp"),
    )
    return jax.shard_map(local, mesh=mesh, in_specs=in_specs, out_specs=out_specs, check_vma=False)
```

```python
import jax
import jax.numpy as jnp
from jax import lax
from jax.sharding import PartitionSpec as P


def swiglu_parts(gate_sum, up_sum, back_sum):
    logistic = jax.nn.sigmoid(gate_sum)
    activated = gate_sum * logistic
    hidden = (activated * up_sum).astype(jnp.bfloat16)
    gate_delta = (back_sum * up_sum * logistic * (1.0 + gate_sum * (1.0 - logistic))).astype(
        jnp.bfloat16
    )
    up_delta = (back_sum * activated).astype(jnp.bfloat16)
    return (hidden, gate_delta, up_delta)


def split_f32(value):
    high = value.astype(jnp.bfloat16)
    rest = value - high.astype(jnp.float32)
    middle = rest.astype(jnp.bfloat16)
    low = (rest - middle.astype(jnp.float32)).astype(jnp.bfloat16)
    return high, middle, low


def local(tokens, out_grad, expert_ids, route_weights, gate_weight, up_weight, down_weight):
    token_count, width_dev = tokens.shape
    per_token = expert_ids.shape[1]
    local_experts = gate_weight.shape[0]
    hidden_units = gate_weight.shape[2]
    sources = lax.axis_size("expert")
    experts = local_experts * sources
    capacity = 2 * token_count * per_token // experts
    slot_count = token_count * per_token
    me = lax.axis_index("expert")

    high, middle, low = split_f32(route_weights)
    route_cols = 4 * per_token
    pad_cols = (-route_cols) % 128
    packed = jnp.concatenate(
        [
            tokens,
            out_grad,
            expert_ids.astype(jnp.bfloat16),
            high,
            middle,
            low,
            jnp.zeros((token_count, pad_cols), jnp.bfloat16),
        ],
        axis=1,
    )
    gathered = lax.all_to_all(
        jnp.broadcast_to(packed[None], (sources,) + packed.shape).reshape(
            sources * token_count, packed.shape[1]
        ),
        "expert",
        split_axis=0,
        concat_axis=0,
        tiled=True,
    )
    feats = gathered[:, : 2 * width_dev]
    route_all = gathered[:, 2 * width_dev : 2 * width_dev + route_cols].astype(jnp.float32)
    ids_all = route_all[:, :per_token].astype(jnp.int32)
    w_all = (
        route_all[:, per_token : 2 * per_token] + route_all[:, 2 * per_token : 3 * per_token]
    ) + route_all[:, 3 * per_token :]
    all_tokens = sources * token_count

    flat_all = ids_all.reshape(sources, slot_count)
    position = jnp.arange(slot_count, dtype=jnp.int32)
    earlier = (flat_all[:, None, :] == flat_all[:, :, None]) & (
        position[None, None, :] < position[None, :, None]
    )
    rank_all = jnp.sum(earlier.astype(jnp.int32), axis=2)
    local_e = flat_all - me * local_experts
    is_local = (local_e >= 0) & (local_e < local_experts)
    src = jnp.arange(sources, dtype=jnp.int32)[:, None]
    row_count = local_experts * sources * capacity
    row_of = jnp.where(is_local, (local_e * sources + src) * capacity + rank_all, row_count)
    row_of = row_of.reshape(sources * slot_count)
    token_of = jnp.arange(sources * slot_count, dtype=jnp.int32) // per_token
    target = jnp.arange(row_count, dtype=jnp.int32)
    hit = target[:, None] == row_of[None, :]
    holder = jnp.sum(jnp.where(hit, token_of[None, :] + 1, 0), axis=1) - 1
    row_weight = jnp.sum(jnp.where(hit, w_all.reshape(-1)[None, :], 0.0), axis=1)
    select = (holder[:, None] == jnp.arange(all_tokens, dtype=jnp.int32)[None, :]).astype(
        jnp.bfloat16
    )
    picked = jnp.dot(select, feats, preferred_element_type=jnp.float32)
    x_in = picked[:, :width_dev].astype(jnp.bfloat16)
    dy_in = (row_weight[:, None] * picked[:, width_dev:]).astype(jnp.bfloat16)
    x_in = x_in.reshape(local_experts, sources * capacity, width_dev)
    dy_in = dy_in.reshape(local_experts, sources * capacity, width_dev)

    gate_part = jnp.einsum(
        "jrd,jdf->jrf", x_in, gate_weight, preferred_element_type=jnp.float32
    ).astype(jnp.bfloat16)
    up_part = jnp.einsum(
        "jrd,jdf->jrf", x_in, up_weight, preferred_element_type=jnp.float32
    ).astype(jnp.bfloat16)
    front = jnp.concatenate([gate_part, up_part], axis=2).reshape(row_count, 2 * hidden_units)
    front_sums = lax.psum_scatter(front, "dp", scatter_dimension=0, tiled=True)
    back_part = jnp.einsum(
        "jrd,jfd->jrf", dy_in, down_weight, preferred_element_type=jnp.float32
    ).astype(jnp.bfloat16)
    dp_count = lax.axis_size("dp")
    back_blocks = lax.all_to_all(
        back_part.reshape(row_count, hidden_units), "dp", split_axis=0, concat_axis=0, tiled=True
    )
    back_sums = jnp.sum(
        back_blocks.reshape(dp_count, row_count // dp_count, hidden_units).astype(jnp.float32),
        axis=0,
    )
    front_sums = front_sums.astype(jnp.float32)
    hidden, gate_delta, up_delta = swiglu_parts(
        front_sums[:, :hidden_units], front_sums[:, hidden_units:], back_sums
    )
    hidden = lax.all_gather(hidden, "dp", axis=0, tiled=True)
    deltas = lax.all_gather(
        jnp.concatenate([gate_delta, up_delta], axis=1), "dp", axis=0, tiled=True
    )
    expert_shape = (local_experts, sources, capacity, hidden_units)
    hidden = hidden.reshape(expert_shape)
    gate_delta = deltas[:, :hidden_units].reshape(expert_shape)
    up_delta = deltas[:, hidden_units:].reshape(expert_shape)
    rows_shape = (local_experts, sources * capacity, hidden_units)

    buffer_rows = experts * capacity
    expert_out = jnp.einsum(
        "jrf,jfd->jrd", hidden.reshape(rows_shape), down_weight, preferred_element_type=jnp.float32
    ).astype(jnp.bfloat16)
    expert_out = expert_out.reshape(local_experts, sources, capacity, width_dev).transpose(1, 0, 2, 3)
    out_back = lax.all_to_all(
        expert_out.reshape(buffer_rows, width_dev), "expert", split_axis=0, concat_axis=0, tiled=True
    )
    down_grad = jnp.einsum(
        "jrf,jrd->jfd", hidden.reshape(rows_shape), dy_in, preferred_element_type=jnp.float32
    ).astype(jnp.bfloat16)
    expert_back = (
        jnp.einsum(
            "jrf,jdf->jrd", gate_delta.reshape(rows_shape), gate_weight,
            preferred_element_type=jnp.float32,
        )
        + jnp.einsum(
            "jrf,jdf->jrd", up_delta.reshape(rows_shape), up_weight,
            preferred_element_type=jnp.float32,
        )
    ).astype(jnp.bfloat16)
    expert_back = expert_back.reshape(local_experts, sources, capacity, width_dev).transpose(
        1, 0, 2, 3
    )
    grad_back = lax.all_to_all(
        expert_back.reshape(buffer_rows, width_dev), "expert", split_axis=0, concat_axis=0, tiled=True
    )
    gate_grad = jnp.einsum(
        "jrd,jrf->jdf", x_in, gate_delta.reshape(rows_shape), preferred_element_type=jnp.float32
    ).astype(jnp.bfloat16)
    up_grad = jnp.einsum(
        "jrd,jrf->jdf", x_in, up_delta.reshape(rows_shape), preferred_element_type=jnp.float32
    ).astype(jnp.bfloat16)

    flat_ids = expert_ids.reshape(slot_count)
    earlier_local = (flat_ids[None, :] == flat_ids[:, None]) & (
        position[None, :] < position[:, None]
    )
    slot_rank = jnp.sum(earlier_local.astype(jnp.int32), axis=1)
    slot_place = (flat_ids * capacity + slot_rank).reshape(token_count, per_token)
    hit_place = slot_place[:, :, None] == jnp.arange(buffer_rows, dtype=jnp.int32)[None, None, :]
    gather_back = jnp.sum(hit_place.astype(jnp.float32), axis=1).astype(jnp.bfloat16)
    gather_out = jnp.sum(jnp.where(hit_place, route_weights[:, :, None], 0.0), axis=1)
    layer_out = jnp.dot(
        gather_out, out_back.astype(jnp.float32), precision=lax.Precision.HIGHEST
    ).astype(jnp.bfloat16)
    grad_tokens = jnp.dot(gather_back, grad_back, preferred_element_type=jnp.float32).astype(
        jnp.bfloat16
    )
    return (layer_out, grad_tokens, gate_grad, up_grad, down_grad)


def solution(mesh):
    in_specs = (
        P("expert", "dp"),
        P("expert", "dp"),
        P("expert", None),
        P("expert", None),
        P("expert", "dp", None),
        P("expert", "dp", None),
        P("expert", None, "dp"),
    )
    out_specs = (
        P("expert", "dp"),
        P("expert", "dp"),
        P("expert", "dp", None),
        P("expert", "dp", None),
        P("expert", None, "dp"),
    )
    return jax.shard_map(local, mesh=mesh, in_specs=in_specs, out_specs=out_specs, check_vma=False)
```

```python
import jax
import jax.numpy as jnp
from jax import lax
from jax.sharding import PartitionSpec as P


def swiglu_parts(gate_sum, up_sum, back_sum):
    logistic = jax.nn.sigmoid(gate_sum)
    activated = gate_sum * logistic
    hidden = (activated * up_sum).astype(jnp.bfloat16)
    gate_delta = (back_sum * up_sum * logistic * (1.0 + gate_sum * (1.0 - logistic))).astype(
        jnp.bfloat16
    )
    up_delta = (back_sum * activated).astype(jnp.bfloat16)
    return (hidden, gate_delta, up_delta)


def split_f32(value):
    high = value.astype(jnp.bfloat16)
    rest = value - high.astype(jnp.float32)
    middle = rest.astype(jnp.bfloat16)
    low = (rest - middle.astype(jnp.float32)).astype(jnp.bfloat16)
    return high, middle, low


def local(tokens, out_grad, expert_ids, route_weights, gate_weight, up_weight, down_weight):
    token_count, width_dev = tokens.shape
    per_token = expert_ids.shape[1]
    local_experts = gate_weight.shape[0]
    hidden_units = gate_weight.shape[2]
    sources = lax.axis_size("expert")
    experts = local_experts * sources
    capacity = 2 * token_count * per_token // experts
    slot_count = token_count * per_token
    me = lax.axis_index("expert")

    high, middle, low = split_f32(route_weights)
    route_cols = 4 * per_token
    pad_cols = (-route_cols) % 128
    packed = jnp.concatenate(
        [
            tokens,
            out_grad,
            expert_ids.astype(jnp.bfloat16),
            high,
            middle,
            low,
            jnp.zeros((token_count, pad_cols), jnp.bfloat16),
        ],
        axis=1,
    )
    gathered = lax.all_to_all(
        jnp.broadcast_to(packed[None], (sources,) + packed.shape).reshape(
            sources * token_count, packed.shape[1]
        ),
        "expert",
        split_axis=0,
        concat_axis=0,
        tiled=True,
    )
    feats = gathered[:, : 2 * width_dev]
    route_all = gathered[:, 2 * width_dev : 2 * width_dev + route_cols].astype(jnp.float32)
    ids_all = route_all[:, :per_token].astype(jnp.int32)
    w_all = (
        route_all[:, per_token : 2 * per_token] + route_all[:, 2 * per_token : 3 * per_token]
    ) + route_all[:, 3 * per_token :]
    all_tokens = sources * token_count

    flat_all = ids_all.reshape(sources, slot_count)
    position = jnp.arange(slot_count, dtype=jnp.int32)
    earlier = (flat_all[:, None, :] == flat_all[:, :, None]) & (
        position[None, None, :] < position[None, :, None]
    )
    rank_all = jnp.sum(earlier.astype(jnp.int32), axis=2)
    local_e = flat_all - me * local_experts
    is_local = (local_e >= 0) & (local_e < local_experts)
    src = jnp.arange(sources, dtype=jnp.int32)[:, None]
    row_count = local_experts * sources * capacity
    row_of = jnp.where(is_local, (local_e * sources + src) * capacity + rank_all, row_count)
    row_of = row_of.reshape(sources * slot_count)
    token_of = jnp.arange(sources * slot_count, dtype=jnp.int32) // per_token
    target = jnp.arange(row_count, dtype=jnp.int32)
    hit = target[:, None] == row_of[None, :]
    holder = jnp.sum(jnp.where(hit, token_of[None, :] + 1, 0), axis=1) - 1
    row_weight = jnp.sum(jnp.where(hit, w_all.reshape(-1)[None, :], 0.0), axis=1)
    select = (holder[:, None] == jnp.arange(all_tokens, dtype=jnp.int32)[None, :]).astype(
        jnp.bfloat16
    )
    picked = jnp.dot(select, feats, preferred_element_type=jnp.float32)
    x_in = picked[:, :width_dev].astype(jnp.bfloat16)
    dy_in = (row_weight[:, None] * picked[:, width_dev:]).astype(jnp.bfloat16)
    x_in = x_in.reshape(local_experts, sources * capacity, width_dev)
    dy_in = dy_in.reshape(local_experts, sources * capacity, width_dev)

    gate_part = jnp.einsum(
        "jrd,jdf->jrf", x_in, gate_weight, preferred_element_type=jnp.float32
    ).astype(jnp.bfloat16)
    up_part = jnp.einsum(
        "jrd,jdf->jrf", x_in, up_weight, preferred_element_type=jnp.float32
    ).astype(jnp.bfloat16)
    front = jnp.concatenate([gate_part, up_part], axis=2).reshape(row_count, 2 * hidden_units)
    front_sums = lax.psum_scatter(front, "dp", scatter_dimension=0, tiled=True)
    back_part = jnp.einsum(
        "jrd,jfd->jrf", dy_in, down_weight, preferred_element_type=jnp.float32
    ).astype(jnp.bfloat16)
    dp_count = lax.axis_size("dp")
    back_blocks = lax.all_to_all(
        back_part.reshape(row_count, hidden_units), "dp", split_axis=0, concat_axis=0, tiled=True
    )
    back_sums = jnp.sum(
        back_blocks.reshape(dp_count, row_count // dp_count, hidden_units).astype(jnp.float32),
        axis=0,
    )
    front_sums = front_sums.astype(jnp.float32)
    hidden, gate_delta, up_delta = swiglu_parts(
        front_sums[:, :hidden_units], front_sums[:, hidden_units:], back_sums
    )
    def dp_gather(block):
        return lax.all_to_all(
            jnp.broadcast_to(block[None], (dp_count,) + block.shape).reshape(
                dp_count * block.shape[0], block.shape[1]
            ),
            "dp",
            split_axis=0,
            concat_axis=0,
            tiled=True,
        )

    hidden = dp_gather(hidden)
    deltas = dp_gather(jnp.concatenate([gate_delta, up_delta], axis=1))
    expert_shape = (local_experts, sources, capacity, hidden_units)
    hidden = hidden.reshape(expert_shape)
    gate_delta = deltas[:, :hidden_units].reshape(expert_shape)
    up_delta = deltas[:, hidden_units:].reshape(expert_shape)
    rows_shape = (local_experts, sources * capacity, hidden_units)

    buffer_rows = experts * capacity
    expert_out = jnp.einsum(
        "jrf,jfd->jrd", hidden.reshape(rows_shape), down_weight, preferred_element_type=jnp.float32
    ).astype(jnp.bfloat16)
    expert_out = expert_out.reshape(local_experts, sources, capacity, width_dev).transpose(1, 0, 2, 3)
    out_back = lax.all_to_all(
        expert_out.reshape(buffer_rows, width_dev), "expert", split_axis=0, concat_axis=0, tiled=True
    )
    down_grad = jnp.einsum(
        "jrf,jrd->jfd", hidden.reshape(rows_shape), dy_in, preferred_element_type=jnp.float32
    ).astype(jnp.bfloat16)
    expert_back = (
        jnp.einsum(
            "jrf,jdf->jrd", gate_delta.reshape(rows_shape), gate_weight,
            preferred_element_type=jnp.float32,
        )
        + jnp.einsum(
            "jrf,jdf->jrd", up_delta.reshape(rows_shape), up_weight,
            preferred_element_type=jnp.float32,
        )
    ).astype(jnp.bfloat16)
    expert_back = expert_back.reshape(local_experts, sources, capacity, width_dev).transpose(
        1, 0, 2, 3
    )
    grad_back = lax.all_to_all(
        expert_back.reshape(buffer_rows, width_dev), "expert", split_axis=0, concat_axis=0, tiled=True
    )
    gate_grad = jnp.einsum(
        "jrd,jrf->jdf", x_in, gate_delta.reshape(rows_shape), preferred_element_type=jnp.float32
    ).astype(jnp.bfloat16)
    up_grad = jnp.einsum(
        "jrd,jrf->jdf", x_in, up_delta.reshape(rows_shape), preferred_element_type=jnp.float32
    ).astype(jnp.bfloat16)

    flat_ids = expert_ids.reshape(slot_count)
    earlier_local = (flat_ids[None, :] == flat_ids[:, None]) & (
        position[None, :] < position[:, None]
    )
    slot_rank = jnp.sum(earlier_local.astype(jnp.int32), axis=1)
    slot_place = (flat_ids * capacity + slot_rank).reshape(token_count, per_token)
    picked_out = jnp.take(out_back, slot_place, axis=0).astype(jnp.float32)
    layer_out = jnp.sum(picked_out * route_weights[:, :, None], axis=1).astype(jnp.bfloat16)
    picked_back = jnp.take(grad_back, slot_place, axis=0).astype(jnp.float32)
    grad_tokens = jnp.sum(picked_back, axis=1).astype(jnp.bfloat16)
    return (layer_out, grad_tokens, gate_grad, up_grad, down_grad)


def solution(mesh):
    in_specs = (
        P("expert", "dp"),
        P("expert", "dp"),
        P("expert", None),
        P("expert", None),
        P("expert", "dp", None),
        P("expert", "dp", None),
        P("expert", None, "dp"),
    )
    out_specs = (
        P("expert", "dp"),
        P("expert", "dp"),
        P("expert", "dp", None),
        P("expert", "dp", None),
        P("expert", None, "dp"),
    )
    return jax.shard_map(local, mesh=mesh, in_specs=in_specs, out_specs=out_specs, check_vma=False)
```
